32 devices in a mesh: band: 16 (over z, x, core), chan: 2 (over y).
Axes of the slice: x: 2, y: 2, z: 4, core: 2. Of those that a mesh axis runs over, the one named last changes fastest.
Arguments:
- features: bfloat16 [256, 64, 1024], P('chan', 'band'), may hold values from -6 to 6
- depth_kernel: bfloat16 [3, 9, 256], P(None, None, 'chan'), may hold values from -2 to 2
- pointwise: bfloat16 [4, 256, 256], P(None, 'chan'), may hold values from -0.25 to 0.25
- cotangent: bfloat16 [256, 64, 1024], P('chan', 'band'), may hold values from -6 to 6
Outputs:
- output: bfloat16 [256, 64, 1024], P('chan', 'band')
- grad_input: float32 [256, 64, 1024], P('chan', 'band')
- grad_depth: float32 [3, 9, 256], P(None, None, 'chan')
- grad_point: float32 [4, 256, 256], P(None, 'chan')
The draws below stay inside these ranges and needn't reach their ends.
All inputs are finite; a program needn't handle non-finite values.
Results may differ from the reference program's by a relative error of at most 0.0057.
Values may be sent and summed in bfloat16 or wider, within the bound.
No kernel may reach another device: no remote copies, remote signals or barrier semaphores. Data moves between devices by JAX's collectives and lax.ppermute only.
A program may use at most 128 MiB of HBM per device.

```python
import jax
import jax.numpy as jnp
from jax import lax

C = 256
LON = 1024
GSCALE = 1024
LAT = 64
N_CHAN = 2


def raised(values, key, source, target, blocks, factor):
    owner, partner = [(jnp.arange(values.shape[axis_at]) // (values.shape[axis_at] // blocks)).reshape([-1 if axis == axis_at else 1 for axis in range(values.ndim)]) for axis_at in (source, target)]
    chosen = jax.random.permutation(key, blocks)[partner]
    strong = (owner == chosen) | (owner == (partner + blocks // 2) % blocks)
    return jnp.where(strong, factor * values, values)


def level_of(key, shape, split, least, top_value):
    factor_of, own = 1.0, jax.random.fold_in(key, 6)
    for axis_at, shards_of in split:
        steps = jnp.exp(jax.random.uniform(jax.random.fold_in(own, axis_at), (shards_of,), jnp.float32, least / len(split), top_value / len(split)))
        factor_of = factor_of * jnp.repeat(steps, shape[axis_at] // shards_of).reshape([-1 if axis == axis_at else 1 for axis in range(len(shape))])
    return factor_of


def centred(key, extent, spread, bound, cuts=(), dtype=jnp.bfloat16):
    array = jax.random.normal(key, extent, jnp.float32) * spread
    if len(cuts) > 0:
        array = level_of(key, extent, cuts, -0.22, 0.18) * array
    return jnp.clip(array, min=-bound, max=bound).astype(dtype)


def bell_draw_with(key, shape, scale, most, cuts, heavy, dtype=jnp.bfloat16):
    entries = scale * jax.random.normal(key, shape, jnp.float32)
    if cuts:
        entries = entries * level_of(key, shape, cuts, -0.22, 0.18)
    return jnp.clip(raised(entries, jax.random.fold_in(key, 3), *heavy), -most, most).astype(dtype)


def setup_inputs(seed: int = 0) -> dict:
    key_list = jax.random.split(jax.random.key(seed), 5)
    features = centred(key_list[0], (C, LAT, LON), 1.0, 6.0, ((0, 2), (1, 16)))
    depth_kernel = centred(key_list[1], (3, 9, C), 9 ** -0.5, 2.0, ((2, 2),))
    pointwise = bell_draw_with(key_list[2], (4, C, C), (4 * C) ** -0.5, 0.25, ((1, 2),), (1, 2, 2, 2.0))
    cotangent = centred(key_list[3], (C, LAT, LON), 1.0, 6.0, ((0, 2), (1, 16)))
    return dict(features=features, depth_kernel=depth_kernel, pointwise=pointwise, cotangent=cotangent)


dilations = (6, 12, 18)


def window(padded, margin, spacing, row_step, col_step, height):
    first = margin + row_step * spacing
    piece = padded[:, first:first + height, :]
    return jnp.roll(piece, -col_step * spacing, axis=-1)


def widen(field, margin):
    return jnp.pad(field, ((0, 0), (margin, margin), (0, 0)))


def reference(features, depth_kernel, pointwise, cotangent):
    height = features.shape[1]
    chans = features.shape[0]
    group_width = chans // N_CHAN
    feat_wide = widen(features.astype(jnp.float32), 18)
    kernel = depth_kernel.astype(jnp.float32)
    branches = [features]
    for which, spacing in enumerate(dilations):
        total = jnp.zeros(features.shape, jnp.float32)
        for tap_index in range(9):
            row_step = tap_index // 3 - 1
            col_step = tap_index % 3 - 1
            total = total + kernel[which, tap_index][:, None, None] * window(feat_wide, 18, spacing, row_step, col_step, height)
        branches.append(total.astype(jnp.bfloat16))
    stacked = jnp.stack(branches)
    result = jnp.zeros(features.shape, jnp.float32)
    for group in range(N_CHAN):
        low = group * group_width
        block = stacked[:, low:low + group_width].astype(jnp.float32)
        weights = pointwise[:, low:low + group_width].astype(jnp.float32)
        partial_sum = jnp.einsum('bchw,bco->ohw', block, weights).astype(jnp.bfloat16)
        partial_sum = lax.optimization_barrier(partial_sum)
        result = result + partial_sum.astype(jnp.float32)
    output = result.astype(jnp.bfloat16)
    dyf = cotangent.astype(jnp.float32)
    point_f = pointwise.astype(jnp.float32)
    grad_branches = [jnp.einsum('co,ohw->chw', point_f[which], dyf).astype(jnp.bfloat16) for which in range(4)]
    grad_point = jnp.stack([jnp.einsum('chw,ohw->co', stacked[which].astype(jnp.float32), dyf) for which in range(4)]) / GSCALE
    grad_input = grad_branches[0].astype(jnp.float32)
    depth_rows = []
    for which, spacing in enumerate(dilations):
        grad_f = grad_branches[which + 1].astype(jnp.float32)
        grad_wide = widen(grad_f, spacing)
        tap_rows = []
        for tap_index in range(9):
            row_step = tap_index // 3 - 1
            col_step = tap_index % 3 - 1
            grad_input = grad_input + kernel[which, tap_index][:, None, None] * window(grad_wide, spacing, spacing, -row_step, -col_step, height)
            tap_rows.append(jnp.sum(grad_f * window(feat_wide, 18, spacing, row_step, col_step, height), axis=(1, 2)))
        depth_rows.append(jnp.stack(tap_rows))
    grad_depth = jnp.stack(depth_rows) / GSCALE
    return (output, grad_input, grad_depth, grad_point)
```

```python
import jax
import jax.numpy as jnp
from jax import lax
from jax.sharding import PartitionSpec as P

GSCALE = 1024


dilations = (6, 12, 18)


def shifted(block, axis, distance):
    devices = range(lax.axis_size(axis))
    route = [(i - distance, i) for i in devices if i - distance in devices]
    if not route:
        return jnp.zeros_like(block)
    return lax.ppermute(block, axis, route)


def from_device(block, ahead):
    return block if ahead == 0 else shifted(block, "band", -ahead)


def rows_at(field, offset):
    height = field.shape[1]
    ahead, start = divmod(offset, height)
    if start == 0:
        return from_device(field, ahead)
    return jnp.concatenate(
        [from_device(field[:, start:], ahead), from_device(field[:, :start], ahead + 1)], axis=1
    )


def local(features, depth_kernel, pointwise, cotangent):
    kernel = depth_kernel.astype(jnp.float32)
    feat_rows = {0: features}
    for spacing in dilations:
        for side in (-1, 1):
            feat_rows[side * spacing] = rows_at(features, side * spacing)
    feat_rows = {k: v.astype(jnp.float32) for k, v in feat_rows.items()}
    branches = [features]
    for which, spacing in enumerate(dilations):
        total = jnp.zeros(features.shape, jnp.float32)
        for tap_index in range(9):
            row_step = tap_index // 3 - 1
            col_step = tap_index % 3 - 1
            total = total + kernel[which, tap_index][:, None, None] * jnp.roll(
                feat_rows[row_step * spacing], -col_step * spacing, axis=-1
            )
        branches.append(total.astype(jnp.bfloat16))
    stacked = jnp.stack(branches)
    output = lax.psum_scatter(
        jnp.einsum("bchw,bco->ohw", stacked, pointwise, preferred_element_type=jnp.float32).astype(
            jnp.bfloat16
        ),
        "chan",
        scatter_dimension=0,
        tiled=True,
    )
    cot_full = lax.all_gather(cotangent, "chan", axis=0, tiled=True)
    grad_sum = jnp.einsum("bco,ohw->bchw", pointwise, cot_full, preferred_element_type=jnp.float32)
    point_local = jnp.einsum("bchw,ohw->bco", stacked, cot_full, preferred_element_type=jnp.float32)
    grad_branches = grad_sum.astype(jnp.bfloat16)
    grad_input = grad_branches[0].astype(jnp.float32)
    depth_rows = []
    for which, spacing in enumerate(dilations):
        grad_field = grad_branches[which + 1]
        grad_f = grad_field.astype(jnp.float32)
        grad_rows = {0: grad_f}
        for side in (-1, 1):
            grad_rows[side * spacing] = rows_at(grad_field, side * spacing).astype(jnp.float32)
        tap_rows = []
        for tap_index in range(9):
            row_step = tap_index // 3 - 1
            col_step = tap_index % 3 - 1
            grad_input = grad_input + kernel[which, tap_index][:, None, None] * jnp.roll(
                grad_rows[-row_step * spacing], col_step * spacing, axis=-1
            )
            tap_rows.append(
                jnp.sum(
                    grad_f * jnp.roll(feat_rows[row_step * spacing], -col_step * spacing, axis=-1),
                    axis=(1, 2),
                )
            )
        depth_rows.append(jnp.stack(tap_rows))
    depth_local = jnp.stack(depth_rows)
    flat = jnp.concatenate([depth_local.reshape(-1), point_local.reshape(-1)])
    flat = lax.psum(flat, "band")
    depth_total = flat[: depth_local.size].reshape(depth_local.shape)
    point_total = flat[depth_local.size :].reshape(point_local.shape)
    return (output, grad_input, depth_total / GSCALE, point_total / GSCALE)


def solution(mesh):
    return jax.shard_map(
        local,
        mesh=mesh,
        in_specs=(
            P("chan", "band", None),
            P(None, None, "chan"),
            P(None, "chan", None),
            P("chan", "band", None),
        ),
        out_specs=(
            P("chan", "band", None),
            P("chan", "band", None),
            P(None, None, "chan"),
            P(None, "chan", None),
        ),
        check_vma=False,
    )
```

```python
import jax
import jax.numpy as jnp
from jax import lax
from jax.sharding import PartitionSpec as P

GSCALE = 1024


dilations = (6, 12, 18)


def shifted(block, axis, distance):
    devices = range(lax.axis_size(axis))
    route = [(i - distance, i) for i in devices if i - distance in devices]
    if not route:
        return jnp.zeros_like(block)
    return lax.ppermute(block, axis, route)


def from_device(block, ahead):
    return block if ahead == 0 else shifted(block, "band", -ahead)


def rows_at(field, offset):
    height = field.shape[1]
    ahead, start = divmod(offset, height)
    if start == 0:
        return from_device(field, ahead)
    return jnp.concatenate(
        [from_device(field[:, start:], ahead), from_device(field[:, :start], ahead + 1)], axis=1
    )


def band_allreduce(flat):
    count = lax.axis_size("band")
    if count & (count - 1):
        return lax.psum(flat, "band")
    length = flat.shape[0]
    flat = jnp.pad(flat, (0, (-length) % count))
    me = lax.axis_index("band")
    bits = []
    bit = 1
    while bit < count:
        bits.append(bit)
        bit *= 2
    for bit in bits:
        half = flat.shape[0] // 2
        upper = (me // bit) % 2 == 1
        keep = jnp.where(upper, flat[half:], flat[:half])
        give = jnp.where(upper, flat[:half], flat[half:])
        flat = keep + lax.ppermute(give, "band", [(j, j ^ bit) for j in range(count)])
    for bit in reversed(bits):
        other = lax.ppermute(flat, "band", [(j, j ^ bit) for j in range(count)])
        upper = (me // bit) % 2 == 1
        flat = jnp.where(upper, jnp.concatenate([other, flat]), jnp.concatenate([flat, other]))
    return flat[:length]


def chan_order(count, sign):
    me = lax.axis_index("chan")
    return lambda width: jnp.concatenate(
        [((me + sign * s) % count) * width + jnp.arange(width) for s in range(count)]
    )


def chan_shift(block, s):
    count = lax.axis_size("chan")
    return lax.ppermute(block, "chan", [(j, (j + s) % count) for j in range(count)])


def local(features, depth_kernel, pointwise, cotangent):
    kernel = depth_kernel.astype(jnp.float32)
    feat_rows = {0: features}
    for spacing in dilations:
        for side in (-1, 1):
            feat_rows[side * spacing] = rows_at(features, side * spacing)
    feat_rows = {k: v.astype(jnp.float32) for k, v in feat_rows.items()}
    branches = [features]
    for which, spacing in enumerate(dilations):
        total = jnp.zeros(features.shape, jnp.float32)
        for tap_index in range(9):
            row_step = tap_index // 3 - 1
            col_step = tap_index % 3 - 1
            total = total + kernel[which, tap_index][:, None, None] * jnp.roll(
                feat_rows[row_step * spacing], -col_step * spacing, axis=-1
            )
        branches.append(total.astype(jnp.bfloat16))
    stacked = jnp.stack(branches)
    count = lax.axis_size("chan")
    width = pointwise.shape[2] // count
    send_order = chan_order(count, 1)(width)
    partial = jnp.einsum(
        "bchw,bco->ohw", stacked, jnp.take(pointwise, send_order, axis=2),
        preferred_element_type=jnp.float32,
    ).astype(jnp.bfloat16)
    result = partial[:width].astype(jnp.float32)
    for s in range(1, count):
        result = result + chan_shift(partial[s * width : (s + 1) * width], s).astype(jnp.float32)
    output = result.astype(jnp.bfloat16)
    cot_full = jnp.concatenate([cotangent] + [chan_shift(cotangent, s) for s in range(1, count)], axis=0)
    recv_order = chan_order(count, -1)(width)
    pw_recv = jnp.take(pointwise, recv_order, axis=2)
    grad_sum = jnp.einsum("bco,ohw->bchw", pw_recv, cot_full, preferred_element_type=jnp.float32)
    point_slots = jnp.einsum("bchw,ohw->bco", stacked, cot_full, preferred_element_type=jnp.float32)
    point_local = jnp.zeros_like(point_slots).at[:, :, recv_order].set(point_slots)
    grad_branches = grad_sum.astype(jnp.bfloat16)
    grad_input = grad_branches[0].astype(jnp.float32)
    depth_rows = []
    for which, spacing in enumerate(dilations):
        grad_field = grad_branches[which + 1]
        grad_f = grad_field.astype(jnp.float32)
        grad_rows = {0: grad_f}
        for side in (-1, 1):
            grad_rows[side * spacing] = rows_at(grad_field, side * spacing).astype(jnp.float32)
        tap_rows = []
        for tap_index in range(9):
            row_step = tap_index // 3 - 1
            col_step = tap_index % 3 - 1
            grad_input = grad_input + kernel[which, tap_index][:, None, None] * jnp.roll(
                grad_rows[-row_step * spacing], col_step * spacing, axis=-1
            )
            tap_rows.append(
                jnp.sum(
                    grad_f * jnp.roll(feat_rows[row_step * spacing], -col_step * spacing, axis=-1),
                    axis=(1, 2),
                )
            )
        depth_rows.append(jnp.stack(tap_rows))
    depth_local = jnp.stack(depth_rows)
    flat = jnp.concatenate([depth_local.reshape(-1), point_local.reshape(-1)])
    flat = band_allreduce(flat)
    depth_total = flat[: depth_local.size].reshape(depth_local.shape)
    point_total = flat[depth_local.size :].reshape(point_local.shape)
    return (output, grad_input, depth_total / GSCALE, point_total / GSCALE)


def solution(mesh):
    return jax.shard_map(
        local,
        mesh=mesh,
        in_specs=(
            P("chan", "band", None),
            P(None, None, "chan"),
            P(None, "chan", None),
            P("chan", "band", None),
        ),
        out_specs=(
            P("chan", "band", None),
            P("chan", "band", None),
            P(None, None, "chan"),
            P(None, "chan", None),
        ),
        check_vma=False,
    )
```

```python
import jax
import jax.numpy as jnp
from jax import lax
from jax.sharding import PartitionSpec as P

GSCALE = 1024


dilations = (6, 12, 18)


def shifted(block, axis, distance):
    devices = range(lax.axis_size(axis))
    route = [(i - distance, i) for i in devices if i - distance in devices]
    if not route:
        return jnp.zeros_like(block)
    return lax.ppermute(block, axis, route)


def pieces_of(height, offset):
    ahead, start = divmod(offset, height)
    if start == 0:
        return [(ahead, 0, height)]
    return [(ahead, start, height), (ahead + 1, 0, start)]


def halo_rows(requests):
    groups = {}
    for key, (field, offset) in requests.items():
        for ahead, first, last in pieces_of(field.shape[1], offset):
            groups.setdefault((ahead, last - first), []).append((key, field, first, last))
    got = {}
    for (ahead, rows), members in groups.items():
        blocks = [field[:, first:last] for _, field, first, last in members]
        joined = jnp.concatenate(blocks, axis=0) if len(blocks) > 1 else blocks[0]
        if ahead != 0:
            joined = shifted(joined, "band", -ahead)
        at = 0
        for (key, field, first, last), block in zip(members, blocks):
            got.setdefault(key, []).append((first, joined[at : at + block.shape[0]]))
            at += block.shape[0]
    out = {}
    for key, (field, offset) in requests.items():
        parts = got[key]
        out[key] = parts[0][1] if len(parts) == 1 else jnp.concatenate([p for _, p in parts], axis=1)
    return out


def band_allreduce(flat):
    count = lax.axis_size("band")
    if count & (count - 1):
        return lax.psum(flat, "band")
    length = flat.shape[0]
    flat = jnp.pad(flat, (0, (-length) % count))
    me = lax.axis_index("band")
    bits = []
    bit = 1
    while bit < count:
        bits.append(bit)
        bit *= 2
    for bit in bits:
        half = flat.shape[0] // 2
        upper = (me // bit) % 2 == 1
        keep = jnp.where(upper, flat[half:], flat[:half])
        give = jnp.where(upper, flat[:half], flat[half:])
        flat = keep + lax.ppermute(give, "band", [(j, j ^ bit) for j in range(count)])
    for bit in reversed(bits):
        other = lax.ppermute(flat, "band", [(j, j ^ bit) for j in range(count)])
        upper = (me // bit) % 2 == 1
        flat = jnp.where(upper, jnp.concatenate([other, flat]), jnp.concatenate([flat, other]))
    return flat[:length]


def chan_order(count, sign, width):
    me = lax.axis_index("chan")
    return jnp.concatenate(
        [((me + sign * s) % count) * width + jnp.arange(width) for s in range(count)]
    )


def chan_shift(block, s):
    count = lax.axis_size("chan")
    return lax.ppermute(block, "chan", [(j, (j + s) % count) for j in range(count)])


def local(features, depth_kernel, pointwise, cotangent):
    kernel = depth_kernel.astype(jnp.float32)
    count = lax.axis_size("chan")
    width = pointwise.shape[2] // count
    cot_full = jnp.concatenate([cotangent] + [chan_shift(cotangent, s) for s in range(1, count)], axis=0)
    recv_order = chan_order(count, -1, width)
    pw_recv = jnp.take(pointwise, recv_order, axis=2)
    grad_sum = jnp.einsum("bco,ohw->bchw", pw_recv, cot_full, preferred_element_type=jnp.float32)
    grad_branches = grad_sum.astype(jnp.bfloat16)

    requests = {}
    for which, spacing in enumerate(dilations):
        for side in (-1, 1):
            requests[("f", side * spacing)] = (features, side * spacing)
            requests[("g", which, side * spacing)] = (grad_branches[which + 1], side * spacing)
    halo = halo_rows(requests)

    feat_rows = {0: features.astype(jnp.float32)}
    for spacing in dilations:
        for side in (-1, 1):
            feat_rows[side * spacing] = halo[("f", side * spacing)].astype(jnp.float32)
    branches = [features]
    for which, spacing in enumerate(dilations):
        total = jnp.zeros(features.shape, jnp.float32)
        for tap_index in range(9):
            row_step = tap_index // 3 - 1
            col_step = tap_index % 3 - 1
            total = total + kernel[which, tap_index][:, None, None] * jnp.roll(
                feat_rows[row_step * spacing], -col_step * spacing, axis=-1
            )
        branches.append(total.astype(jnp.bfloat16))
    stacked = jnp.stack(branches)

    send_order = chan_order(count, 1, width)
    partial = jnp.einsum(
        "bchw,bco->ohw", stacked, jnp.take(pointwise, send_order, axis=2),
        preferred_element_type=jnp.float32,
    ).astype(jnp.bfloat16)
    result = partial[:width].astype(jnp.float32)
    for s in range(1, count):
        result = result + chan_shift(partial[s * width : (s + 1) * width], s).astype(jnp.float32)
    output = result.astype(jnp.bfloat16)

    point_slots = jnp.einsum("bchw,ohw->bco", stacked, cot_full, preferred_element_type=jnp.float32)
    point_local = jnp.take(point_slots, recv_order, axis=2)

    grad_input = grad_branches[0].astype(jnp.float32)
    depth_rows = []
    for which, spacing in enumerate(dilations):
        grad_f = grad_branches[which + 1].astype(jnp.float32)
        grad_rows = {0: grad_f}
        for side in (-1, 1):
            grad_rows[side * spacing] = halo[("g", which, side * spacing)].astype(jnp.float32)
        tap_rows = []
        for tap_index in range(9):
            row_step = tap_index // 3 - 1
            col_step = tap_index % 3 - 1
            grad_input = grad_input + kernel[which, tap_index][:, None, None] * jnp.roll(
                grad_rows[-row_step * spacing], col_step * spacing, axis=-1
            )
            tap_rows.append(
                jnp.sum(
                    grad_f * jnp.roll(feat_rows[row_step * spacing], -col_step * spacing, axis=-1),
                    axis=(1, 2),
                )
            )
        depth_rows.append(jnp.stack(tap_rows))
    depth_local = jnp.stack(depth_rows)
    flat = jnp.concatenate([depth_local.reshape(-1), point_local.reshape(-1)])
    flat = band_allreduce(flat)
    depth_total = flat[: depth_local.size].reshape(depth_local.shape)
    point_total = flat[depth_local.size :].reshape(point_local.shape)
    return (output, grad_input, depth_total / GSCALE, point_total / GSCALE)


def solution(mesh):
    return jax.shard_map(
        local,
        mesh=mesh,
        in_specs=(
            P("chan", "band", None),
            P(None, None, "chan"),
            P(None, "chan", None),
            P("chan", "band", None),
        ),
        out_specs=(
            P("chan", "band", None),
            P("chan", "band", None),
            P(None, None, "chan"),
            P(None, "chan", None),
        ),
        check_vma=False,
    )
```

```python
import jax
import jax.numpy as jnp
from jax import lax
from jax.sharding import PartitionSpec as P


GSCALE = 1024


dilations = (6, 12, 18)


def shifted(block, axis, distance):
    devices = range(lax.axis_size(axis))
    route = [(i - distance, i) for i in devices if i - distance in devices]
    if not route:
        return jnp.zeros_like(block)
    return lax.ppermute(block, axis, route)


def pieces_of(height, offset):
    ahead, start = divmod(offset, height)
    if start == 0:
        return [(ahead, 0, height)]
    return [(ahead, start, height), (ahead + 1, 0, start)]


def halo_rows(requests):
    groups = {}
    for key, (field, offset) in requests.items():
        for ahead, first, last in pieces_of(field.shape[1], offset):
            groups.setdefault((ahead, last - first), []).append((key, field, first, last))
    got = {}
    for (ahead, rows), members in groups.items():
        blocks = [field[:, first:last] for _, field, first, last in members]
        joined = jnp.concatenate(blocks, axis=0) if len(blocks) > 1 else blocks[0]
        if ahead != 0:
            joined = shifted(joined, "band", -ahead)
        at = 0
        for (key, field, first, last), block in zip(members, blocks):
            got.setdefault(key, []).append((first, joined[at : at + block.shape[0]]))
            at += block.shape[0]
    out = {}
    for key, (field, offset) in requests.items():
        parts = got[key]
        out[key] = parts[0][1] if len(parts) == 1 else jnp.concatenate([p for _, p in parts], axis=1)
    return out


def chan_order(count, sign, width):
    me = lax.axis_index("chan")
    return jnp.concatenate(
        [((me + sign * s) % count) * width + jnp.arange(width) for s in range(count)]
    )


def chan_shift(block, s):
    count = lax.axis_size("chan")
    return lax.ppermute(block, "chan", [(j, (j + s) % count) for j in range(count)])


def block(features, depth_kernel, pointwise, cotangent):
    kernel = depth_kernel.astype(jnp.float32)
    count = lax.axis_size("chan")
    width = pointwise.shape[2] // count
    cot_full = jnp.concatenate(
        [cotangent] + [chan_shift(cotangent, s) for s in range(1, count)], axis=0
    )
    requests = {}
    for spacing in dilations:
        for side in (-1, 1):
            requests[side * spacing] = (features, side * spacing)
    feat_halo = halo_rows(requests)
    recv_order = chan_order(count, -1, width)
    pw_recv = jnp.take(pointwise, recv_order, axis=2)
    grad_sum = jnp.einsum("bco,ohw->bchw", pw_recv, cot_full, preferred_element_type=jnp.float32)
    grad_branches = grad_sum.astype(jnp.bfloat16)
    requests = {}
    for which, spacing in enumerate(dilations):
        for side in (-1, 1):
            requests[(which, side * spacing)] = (grad_branches[which + 1], side * spacing)
    grad_halo = halo_rows(requests)

    feat_rows = {0: features.astype(jnp.float32)}
    for offset, rows in feat_halo.items():
        feat_rows[offset] = rows.astype(jnp.float32)
    branches = [features]
    for which, spacing in enumerate(dilations):
        total = jnp.zeros(features.shape, jnp.float32)
        for tap_index in range(9):
            row_step = tap_index // 3 - 1
            col_step = tap_index % 3 - 1
            total = total + kernel[which, tap_index][:, None, None] * jnp.roll(
                feat_rows[row_step * spacing], -col_step * spacing, axis=-1
            )
        branches.append(total.astype(jnp.bfloat16))
    stacked = jnp.stack(branches)

    send_order = chan_order(count, 1, width)
    partial = jnp.einsum(
        "bchw,bco->ohw", stacked, jnp.take(pointwise, send_order, axis=2),
        preferred_element_type=jnp.float32,
    ).astype(jnp.bfloat16)
    result = partial[:width].astype(jnp.float32)
    for s in range(1, count):
        result = result + chan_shift(partial[s * width : (s + 1) * width], s).astype(jnp.float32)
    output = result.astype(jnp.bfloat16)

    point_slots = jnp.einsum("bchw,ohw->bco", stacked, cot_full, preferred_element_type=jnp.float32)
    point_local = jnp.take(point_slots, recv_order, axis=2)

    grad_input = grad_branches[0].astype(jnp.float32)
    depth_rows = []
    for which, spacing in enumerate(dilations):
        grad_f = grad_branches[which + 1].astype(jnp.float32)
        grad_rows = {0: grad_f}
        for side in (-1, 1):
            grad_rows[side * spacing] = grad_halo[(which, side * spacing)].astype(jnp.float32)
        tap_rows = []
        for tap_index in range(9):
            row_step = tap_index // 3 - 1
            col_step = tap_index % 3 - 1
            grad_input = grad_input + kernel[which, tap_index][:, None, None] * jnp.roll(
                grad_rows[-row_step * spacing], col_step * spacing, axis=-1
            )
            tap_rows.append(
                jnp.sum(
                    grad_f * jnp.roll(feat_rows[row_step * spacing], -col_step * spacing, axis=-1),
                    axis=(1, 2),
                )
            )
        depth_rows.append(jnp.stack(tap_rows))
    depth_local = jnp.stack(depth_rows)
    flat = jnp.concatenate([depth_local.reshape(-1), point_local.reshape(-1)])
    flat = lax.psum(flat, "band")
    depth_total = flat[: depth_local.size].reshape(depth_local.shape)
    point_total = flat[depth_local.size :].reshape(point_local.shape)
    return (output, grad_input, depth_total / GSCALE, point_total / GSCALE)


def solution(mesh):
    return jax.shard_map(
        block,
        mesh=mesh,
        in_specs=(
            P("chan", "band", None),
            P(None, None, "chan"),
            P(None, "chan", None),
            P("chan", "band", None),
        ),
        out_specs=(
            P("chan", "band", None),
            P("chan", "band", None),
            P(None, None, "chan"),
            P(None, "chan", None),
        ),
        check_vma=False,
    )
```

```python
import jax
import jax.numpy as jnp
from jax import lax
from jax.sharding import PartitionSpec as P


GSCALE = 1024


dilations = (6, 12, 18)


def shifted(block, axis, distance):
    devices = range(lax.axis_size(axis))
    route = [(i - distance, i) for i in devices if i - distance in devices]
    if not route:
        return jnp.zeros_like(block)
    return lax.ppermute(block, axis, route)


def pieces_of(height, offset):
    ahead, start = divmod(offset, height)
    if start == 0:
        return [(ahead, 0, height)]
    return [(ahead, start, height), (ahead + 1, 0, start)]


def halo_rows(requests):
    groups = {}
    for key, (field, offset) in requests.items():
        for ahead, first, last in pieces_of(field.shape[1], offset):
            groups.setdefault((ahead, last - first), []).append((key, field, first, last))
    got = {}
    for (ahead, rows), members in groups.items():
        blocks = [field[:, first:last] for _, field, first, last in members]
        joined = jnp.concatenate(blocks, axis=0) if len(blocks) > 1 else blocks[0]
        if ahead != 0:
            joined = shifted(joined, "band", -ahead)
        at = 0
        for (key, field, first, last), block in zip(members, blocks):
            got.setdefault(key, []).append((first, joined[at : at + block.shape[0]]))
            at += block.shape[0]
    out = {}
    for key, (field, offset) in requests.items():
        parts = got[key]
        out[key] = parts[0][1] if len(parts) == 1 else jnp.concatenate([p for _, p in parts], axis=1)
    return out


def chan_order(count, sign, width):
    me = lax.axis_index("chan")
    return jnp.concatenate(
        [((me + sign * s) % count) * width + jnp.arange(width) for s in range(count)]
    )


def chan_shift(block, s):
    count = lax.axis_size("chan")
    return lax.ppermute(block, "chan", [(j, (j + s) % count) for j in range(count)])


def block(features, depth_kernel, pointwise, cotangent):
    kernel = depth_kernel.astype(jnp.float32)
    count = lax.axis_size("chan")
    width = pointwise.shape[2] // count
    cot_full = jnp.concatenate(
        [cotangent] + [chan_shift(cotangent, s) for s in range(1, count)], axis=0
    )
    requests = {}
    for spacing in dilations:
        for side in (-1, 1):
            requests[side * spacing] = (features, side * spacing)
    feat_halo = halo_rows(requests)
    recv_order = chan_order(count, -1, width)
    pw_recv = jnp.take(pointwise, recv_order, axis=2)
    grad_sum = jnp.einsum("bco,ohw->bchw", pw_recv, cot_full, preferred_element_type=jnp.float32)
    grad_branches = grad_sum.astype(jnp.bfloat16)
    requests = {}
    for which, spacing in enumerate(dilations):
        for side in (-1, 1):
            requests[(which, side * spacing)] = (grad_branches[which + 1], side * spacing)
    grad_halo = halo_rows(requests)

    feat_rows = {0: features.astype(jnp.float32)}
    for offset, rows in feat_halo.items():
        feat_rows[offset] = rows.astype(jnp.float32)
    branches = [features]
    for which, spacing in enumerate(dilations):
        total = jnp.zeros(features.shape, jnp.float32)
        for tap_index in range(9):
            row_step = tap_index // 3 - 1
            col_step = tap_index % 3 - 1
            total = total + kernel[which, tap_index][:, None, None] * jnp.roll(
                feat_rows[row_step * spacing], -col_step * spacing, axis=-1
            )
        branches.append(total.astype(jnp.bfloat16))
    stacked = jnp.stack(branches)

    send_order = chan_order(count, 1, width)
    partial = jnp.einsum(
        "bchw,bco->ohw", stacked, jnp.take(pointwise, send_order, axis=2),
        preferred_element_type=jnp.float32,
    ).astype(jnp.bfloat16)
    result = partial[:width].astype(jnp.float32)
    for s in range(1, count):
        result = result + chan_shift(partial[s * width : (s + 1) * width], s).astype(jnp.float32)
    output = result.astype(jnp.bfloat16)

    point_slots = jnp.einsum("bchw,ohw->bco", stacked, cot_full, preferred_element_type=jnp.float32)
    point_local = jnp.take(point_slots, recv_order, axis=2)

    depth_rows = []
    for which, spacing in enumerate(dilations):
        grad_f = grad_branches[which + 1].astype(jnp.float32)
        tap_rows = []
        for tap_index in range(9):
            row_step = tap_index // 3 - 1
            col_step = tap_index % 3 - 1
            tap_rows.append(
                jnp.sum(
                    grad_f * jnp.roll(feat_rows[row_step * spacing], -col_step * spacing, axis=-1),
                    axis=(1, 2),
                )
            )
        depth_rows.append(jnp.stack(tap_rows))
    depth_local = jnp.stack(depth_rows)
    flat = jnp.concatenate([depth_local.reshape(-1), point_local.reshape(-1)])
    flat = lax.psum(flat, "band")
    depth_total = flat[: depth_local.size].reshape(depth_local.shape)
    point_total = flat[depth_local.size :].reshape(point_local.shape)

    grad_input = grad_branches[0].astype(jnp.float32)
    for which, spacing in enumerate(dilations):
        grad_rows = {0: grad_branches[which + 1].astype(jnp.float32)}
        for side in (-1, 1):
            grad_rows[side * spacing] = grad_halo[(which, side * spacing)].astype(jnp.float32)
        for tap_index in range(9):
            row_step = tap_index // 3 - 1
            col_step = tap_index % 3 - 1
            grad_input = grad_input + kernel[which, tap_index][:, None, None] * jnp.roll(
                grad_rows[-row_step * spacing], col_step * spacing, axis=-1
            )
    return (output, grad_input, depth_total / GSCALE, point_total / GSCALE)


def solution(mesh):
    return jax.shard_map(
        block,
        mesh=mesh,
        in_specs=(
            P("chan", "band", None),
            P(None, None, "chan"),
            P(None, "chan", None),
            P("chan", "band", None),
        ),
        out_specs=(
            P("chan", "band", None),
            P("chan", "band", None),
            P(None, None, "chan"),
            P(None, "chan", None),
        ),
        check_vma=False,
    )
```

```python
import jax
import jax.numpy as jnp
from jax import lax
from jax.sharding import PartitionSpec as P


GSCALE = 1024


dilations = (6, 12, 18)


def shifted(block, axis, distance):
    devices = range(lax.axis_size(axis))
    route = [(i - distance, i) for i in devices if i - distance in devices]
    if not route:
        return jnp.zeros_like(block)
    return lax.ppermute(block, axis, route)


def pieces_of(height, offset):
    ahead, start = divmod(offset, height)
    if start == 0:
        return [(ahead, 0, height)]
    return [(ahead, start, height), (ahead + 1, 0, start)]


def halo_rows(requests):
    groups = {}
    for key, (field, offset) in requests.items():
        for ahead, first, last in pieces_of(field.shape[1], offset):
            groups.setdefault((ahead, last - first), []).append((key, field, first, last))
    got = {}
    for (ahead, rows), members in groups.items():
        blocks = [field[:, first:last] for _, field, first, last in members]
        joined = jnp.concatenate(blocks, axis=0) if len(blocks) > 1 else blocks[0]
        if ahead != 0:
            joined = shifted(joined, "band", -ahead)
        at = 0
        for (key, field, first, last), block in zip(members, blocks):
            got.setdefault(key, []).append((first, joined[at : at + block.shape[0]]))
            at += block.shape[0]
    out = {}
    for key, (field, offset) in requests.items():
        parts = got[key]
        out[key] = parts[0][1] if len(parts) == 1 else jnp.concatenate([p for _, p in parts], axis=1)
    return out


def chan_shift(block, s):
    count = lax.axis_size("chan")
    return lax.ppermute(block, "chan", [(j, (j + s) % count) for j in range(count)])


def block(features, depth_kernel, pointwise, cotangent):
    kernel = depth_kernel.astype(jnp.float32)
    count = lax.axis_size("chan")
    width = pointwise.shape[2] // count
    cot_full = jnp.concatenate(
        [cotangent] + [chan_shift(cotangent, s) for s in range(1, count)], axis=0
    )
    requests = {}
    for spacing in dilations:
        for side in (-1, 1):
            requests[side * spacing] = (features, side * spacing)
    feat_halo = halo_rows(requests)
    me = lax.axis_index("chan")
    pw_slots = [
        lax.dynamic_slice_in_dim(pointwise, ((me - s) % count) * width, width, axis=2)
        for s in range(count)
    ]
    grad_sum = sum(
        jnp.einsum(
            "bco,ohw->bchw", pw_slots[s], cot_full[s * width : (s + 1) * width],
            preferred_element_type=jnp.float32,
        )
        for s in range(count)
    )
    grad_branches = grad_sum.astype(jnp.bfloat16)
    requests = {}
    for which, spacing in enumerate(dilations):
        for side in (-1, 1):
            requests[(which, side * spacing)] = (grad_branches[which + 1], side * spacing)
    grad_halo = halo_rows(requests)

    feat_rows = {0: features.astype(jnp.float32)}
    for offset, rows in feat_halo.items():
        feat_rows[offset] = rows.astype(jnp.float32)
    branches = [features]
    for which, spacing in enumerate(dilations):
        total = jnp.zeros(features.shape, jnp.float32)
        for tap_index in range(9):
            row_step = tap_index // 3 - 1
            col_step = tap_index % 3 - 1
            total = total + kernel[which, tap_index][:, None, None] * jnp.roll(
                feat_rows[row_step * spacing], -col_step * spacing, axis=-1
            )
        branches.append(total.astype(jnp.bfloat16))
    stacked = jnp.stack(branches)

    partial = jnp.einsum(
        "bchw,bco->ohw", stacked, pointwise, preferred_element_type=jnp.float32
    ).astype(jnp.bfloat16)
    result = lax.dynamic_slice_in_dim(partial, me * width, width, axis=0).astype(jnp.float32)
    for s in range(1, count):
        piece = lax.dynamic_slice_in_dim(partial, ((me + s) % count) * width, width, axis=0)
        result = result + chan_shift(piece, s).astype(jnp.float32)
    output = result.astype(jnp.bfloat16)

    point_local = jnp.zeros(pointwise.shape, jnp.float32)
    for s in range(count):
        point_slot = jnp.einsum(
            "bchw,ohw->bco", stacked, cot_full[s * width : (s + 1) * width],
            preferred_element_type=jnp.float32,
        )
        point_local = lax.dynamic_update_slice_in_dim(
            point_local, point_slot, ((me - s) % count) * width, axis=2
        )

    depth_rows = []
    for which, spacing in enumerate(dilations):
        grad_f = grad_branches[which + 1].astype(jnp.float32)
        tap_rows = []
        for tap_index in range(9):
            row_step = tap_index // 3 - 1
            col_step = tap_index % 3 - 1
            tap_rows.append(
                jnp.sum(
                    grad_f * jnp.roll(feat_rows[row_step * spacing], -col_step * spacing, axis=-1),
                    axis=(1, 2),
                )
            )
        depth_rows.append(jnp.stack(tap_rows))
    depth_local = jnp.stack(depth_rows)
    flat = jnp.concatenate([depth_local.reshape(-1), point_local.reshape(-1)])
    flat = lax.psum(flat, "band")
    depth_total = flat[: depth_local.size].reshape(depth_local.shape)
    point_total = flat[depth_local.size :].reshape(point_local.shape)

    grad_input = grad_branches[0].astype(jnp.float32)
    for which, spacing in enumerate(dilations):
        grad_rows = {0: grad_branches[which + 1].astype(jnp.float32)}
        for side in (-1, 1):
            grad_rows[side * spacing] = grad_halo[(which, side * spacing)].astype(jnp.float32)
        for tap_index in range(9):
            row_step = tap_index // 3 - 1
            col_step = tap_index % 3 - 1
            grad_input = grad_input + kernel[which, tap_index][:, None, None] * jnp.roll(
                grad_rows[-row_step * spacing], col_step * spacing, axis=-1
            )
    return (output, grad_input, depth_total / GSCALE, point_total / GSCALE)


def solution(mesh):
    return jax.shard_map(
        block,
        mesh=mesh,
        in_specs=(
            P("chan", "band", None),
            P(None, None, "chan"),
            P(None, "chan", None),
            P("chan", "band", None),
        ),
        out_specs=(
            P("chan", "band", None),
            P("chan", "band", None),
            P(None, None, "chan"),
            P(None, "chan", None),
        ),
        check_vma=False,
    )
```

```python
import jax
import jax.numpy as jnp
from jax import lax
from jax.sharding import PartitionSpec as P


GSCALE = 1024


dilations = (6, 12, 18)


def shifted(block, axis, distance):
    devices = range(lax.axis_size(axis))
    route = [(i - distance, i) for i in devices if i - distance in devices]
    if not route:
        return jnp.zeros_like(block)
    return lax.ppermute(block, axis, route)


def pieces_of(height, offset):
    ahead, start = divmod(offset, height)
    if start == 0:
        return [(ahead, 0, height)]
    return [(ahead, start, height), (ahead + 1, 0, start)]


def halo_rows(requests):
    groups = {}
    for key, (field, offset) in requests.items():
        for ahead, first, last in pieces_of(field.shape[1], offset):
            groups.setdefault((ahead, last - first), []).append((key, field, first, last))
    got = {}
    for (ahead, rows), members in groups.items():
        blocks = [field[:, first:last] for _, field, first, last in members]
        joined = jnp.concatenate(blocks, axis=0) if len(blocks) > 1 else blocks[0]
        if ahead != 0:
            joined = shifted(joined, "band", -ahead)
        at = 0
        for (key, field, first, last), block in zip(members, blocks):
            got.setdefault(key, []).append((first, joined[at : at + block.shape[0]]))
            at += block.shape[0]
    out = {}
    for key, (field, offset) in requests.items():
        parts = got[key]
        out[key] = parts[0][1] if len(parts) == 1 else jnp.concatenate([p for _, p in parts], axis=1)
    return out


def band_allreduce(flat):
    count = lax.axis_size("band")
    radices = []
    rest = count
    while rest % 4 == 0:
        radices.append(4)
        rest //= 4
    while rest % 2 == 0:
        radices.append(2)
        rest //= 2
    if rest != 1:
        return lax.psum(flat, "band")
    length = flat.shape[0]
    flat = jnp.pad(flat, (0, (-length) % count))
    me = lax.axis_index("band")
    steps = []
    stride = 1
    for radix in radices:
        steps.append((stride, radix))
        stride *= radix

    def rotate(stride, radix, u):
        return [
            (j, j + (((j // stride) % radix + u) % radix - (j // stride) % radix) * stride)
            for j in range(count)
        ]

    for stride, radix in steps:
        digit = (me // stride) % radix
        size = flat.shape[0] // radix
        acc = lax.dynamic_slice_in_dim(flat, digit * size, size)
        for u in range(1, radix):
            give = lax.dynamic_slice_in_dim(flat, ((digit + u) % radix) * size, size)
            acc = acc + lax.ppermute(give, "band", rotate(stride, radix, u))
        flat = acc
    for stride, radix in reversed(steps):
        digit = (me // stride) % radix
        size = flat.shape[0]
        full = lax.dynamic_update_slice_in_dim(
            jnp.zeros((size * radix,), flat.dtype), flat, digit * size, 0
        )
        for u in range(1, radix):
            got = lax.ppermute(flat, "band", rotate(stride, radix, u))
            full = lax.dynamic_update_slice_in_dim(full, got, ((digit - u) % radix) * size, 0)
        flat = full
    return flat[:length]


def chan_shift(block, s):
    count = lax.axis_size("chan")
    return lax.ppermute(block, "chan", [(j, (j + s) % count) for j in range(count)])


def block(features, depth_kernel, pointwise, cotangent):
    kernel = depth_kernel.astype(jnp.float32)
    count = lax.axis_size("chan")
    width = pointwise.shape[2] // count
    cot_full = jnp.concatenate(
        [cotangent] + [chan_shift(cotangent, s) for s in range(1, count)], axis=0
    )
    requests = {}
    for spacing in dilations:
        for side in (-1, 1):
            requests[side * spacing] = (features, side * spacing)
    feat_halo = halo_rows(requests)
    me = lax.axis_index("chan")
    pw_slots = [
        lax.dynamic_slice_in_dim(pointwise, ((me - s) % count) * width, width, axis=2)
        for s in range(count)
    ]
    grad_sum = sum(
        jnp.einsum(
            "bco,ohw->bchw", pw_slots[s], cot_full[s * width : (s + 1) * width],
            preferred_element_type=jnp.float32,
        )
        for s in range(count)
    )
    grad_branches = grad_sum.astype(jnp.bfloat16)
    requests = {}
    for which, spacing in enumerate(dilations):
        for side in (-1, 1):
            requests[(which, side * spacing)] = (grad_branches[which + 1], side * spacing)
    grad_halo = halo_rows(requests)

    feat_rows = {0: features.astype(jnp.float32)}
    for offset, rows in feat_halo.items():
        feat_rows[offset] = rows.astype(jnp.float32)
    branches = [features]
    for which, spacing in enumerate(dilations):
        total = jnp.zeros(features.shape, jnp.float32)
        for tap_index in range(9):
            row_step = tap_index // 3 - 1
            col_step = tap_index % 3 - 1
            total = total + kernel[which, tap_index][:, None, None] * jnp.roll(
                feat_rows[row_step * spacing], -col_step * spacing, axis=-1
            )
        branches.append(total.astype(jnp.bfloat16))
    stacked = jnp.stack(branches)

    partial = jnp.einsum(
        "bchw,bco->ohw", stacked, pointwise, preferred_element_type=jnp.float32
    ).astype(jnp.bfloat16)
    result = lax.dynamic_slice_in_dim(partial, me * width, width, axis=0).astype(jnp.float32)
    for s in range(1, count):
        piece = lax.dynamic_slice_in_dim(partial, ((me + s) % count) * width, width, axis=0)
        result = result + chan_shift(piece, s).astype(jnp.float32)
    output = result.astype(jnp.bfloat16)

    point_local = jnp.zeros(pointwise.shape, jnp.float32)
    for s in range(count):
        point_slot = jnp.einsum(
            "bchw,ohw->bco", stacked, cot_full[s * width : (s + 1) * width],
            preferred_element_type=jnp.float32,
        )
        point_local = lax.dynamic_update_slice_in_dim(
            point_local, point_slot, ((me - s) % count) * width, axis=2
        )

    depth_rows = []
    for which, spacing in enumerate(dilations):
        grad_f = grad_branches[which + 1].astype(jnp.float32)
        tap_rows = []
        for tap_index in range(9):
            row_step = tap_index // 3 - 1
            col_step = tap_index % 3 - 1
            tap_rows.append(
                jnp.sum(
                    grad_f * jnp.roll(feat_rows[row_step * spacing], -col_step * spacing, axis=-1),
                    axis=(1, 2),
                )
            )
        depth_rows.append(jnp.stack(tap_rows))
    depth_local = jnp.stack(depth_rows)
    flat = jnp.concatenate([depth_local.reshape(-1), point_local.reshape(-1)])
    flat = band_allreduce(flat)
    depth_total = flat[: depth_local.size].reshape(depth_local.shape)
    point_total = flat[depth_local.size :].reshape(point_local.shape)

    grad_input = grad_branches[0].astype(jnp.float32)
    for which, spacing in enumerate(dilations):
        grad_rows = {0: grad_branches[which + 1].astype(jnp.float32)}
        for side in (-1, 1):
            grad_rows[side * spacing] = grad_halo[(which, side * spacing)].astype(jnp.float32)
        for tap_index in range(9):
            row_step = tap_index // 3 - 1
            col_step = tap_index % 3 - 1
            grad_input = grad_input + kernel[which, tap_index][:, None, None] * jnp.roll(
                grad_rows[-row_step * spacing], col_step * spacing, axis=-1
            )
    return (output, grad_input, depth_total / GSCALE, point_total / GSCALE)


def solution(mesh):
    return jax.shard_map(
        block,
        mesh=mesh,
        in_specs=(
            P("chan", "band", None),
            P(None, None, "chan"),
            P(None, "chan", None),
            P("chan", "band", None),
        ),
        out_specs=(
            P("chan", "band", None),
            P("chan", "band", None),
            P(None, None, "chan"),
            P(None, "chan", None),
        ),
        check_vma=False,
    )
```

```python
import jax
import jax.numpy as jnp
from jax import lax
from jax.sharding import PartitionSpec as P


GSCALE = 1024


dilations = (6, 12, 18)


def shifted(block, axis, distance):
    devices = range(lax.axis_size(axis))
    route = [(i - distance, i) for i in devices if i - distance in devices]
    if not route:
        return jnp.zeros_like(block)
    return lax.ppermute(block, axis, route)


def pieces_of(height, offset):
    ahead, start = divmod(offset, height)
    if start == 0:
        return [(ahead, 0, height)]
    return [(ahead, start, height), (ahead + 1, 0, start)]


def halo_rows(requests):
    groups = {}
    for key, (field, offset) in requests.items():
        for ahead, first, last in pieces_of(field.shape[1], offset):
            groups.setdefault((ahead, last - first), []).append((key, field, first, last))
    got = {}
    for (ahead, rows), members in groups.items():
        blocks = [field[:, first:last] for _, field, first, last in members]
        joined = jnp.concatenate(blocks, axis=0) if len(blocks) > 1 else blocks[0]
        if ahead != 0:
            joined = shifted(joined, "band", -ahead)
        at = 0
        for (key, field, first, last), block in zip(members, blocks):
            got.setdefault(key, []).append((first, joined[at : at + block.shape[0]]))
            at += block.shape[0]
    out = {}
    for key, (field, offset) in requests.items():
        parts = got[key]
        out[key] = parts[0][1] if len(parts) == 1 else jnp.concatenate([p for _, p in parts], axis=1)
    return out


def band_allreduce(flat):
    count = lax.axis_size("band")
    radices = []
    rest = count
    while rest % 4 == 0:
        radices.append(4)
        rest //= 4
    while rest % 2 == 0:
        radices.append(2)
        rest //= 2
    if rest != 1:
        return lax.psum(flat, "band")
    length = flat.shape[0]
    flat = jnp.pad(flat, (0, (-length) % count))
    me = lax.axis_index("band")
    steps = []
    stride = 1
    for radix in radices:
        steps.append((stride, radix))
        stride *= radix

    def rotate(stride, radix, u):
        return [
            (j, j + (((j // stride) % radix + u) % radix - (j // stride) % radix) * stride)
            for j in range(count)
        ]

    for stride, radix in steps:
        digit = (me // stride) % radix
        size = flat.shape[0] // radix
        acc = lax.dynamic_slice_in_dim(flat, digit * size, size)
        for u in range(1, radix):
            give = lax.dynamic_slice_in_dim(flat, ((digit + u) % radix) * size, size)
            acc = acc + lax.ppermute(give, "band", rotate(stride, radix, u))
        flat = acc
    for stride, radix in reversed(steps):
        digit = (me // stride) % radix
        size = flat.shape[0]
        full = lax.dynamic_update_slice_in_dim(
            jnp.zeros((size * radix,), flat.dtype), flat, digit * size, 0
        )
        for u in range(1, radix):
            got = lax.ppermute(flat, "band", rotate(stride, radix, u))
            full = lax.dynamic_update_slice_in_dim(full, got, ((digit - u) % radix) * size, 0)
        flat = full
    return flat[:length]


def chan_shift(block, s):
    count = lax.axis_size("chan")
    return lax.ppermute(block, "chan", [(j, (j + s) % count) for j in range(count)])


def block(features, depth_kernel, pointwise, cotangent):
    kernel = depth_kernel.astype(jnp.float32)
    count = lax.axis_size("chan")
    width = pointwise.shape[2] // count
    cot_full = jnp.concatenate(
        [cotangent] + [chan_shift(cotangent, s) for s in range(1, count)], axis=0
    )
    me = lax.axis_index("chan")
    pw_slots = [
        lax.dynamic_slice_in_dim(pointwise, ((me - s) % count) * width, width, axis=2)
        for s in range(count)
    ]
    grad_sum = sum(
        jnp.einsum(
            "bco,ohw->bchw", pw_slots[s], cot_full[s * width : (s + 1) * width],
            preferred_element_type=jnp.float32,
        )
        for s in range(count)
    )
    grad_branches = grad_sum.astype(jnp.bfloat16)
    requests = {}
    for which, spacing in enumerate(dilations):
        for side in (-1, 1):
            requests[("f", side * spacing)] = (features, side * spacing)
            requests[("g", which, side * spacing)] = (grad_branches[which + 1], side * spacing)
    halo = halo_rows(requests)
    grad_halo = {(which, off): halo[("g", which, off)] for which in range(3) for off in (-dilations[which], dilations[which])}

    feat_rows = {0: features.astype(jnp.float32)}
    for spacing in dilations:
        for side in (-1, 1):
            feat_rows[side * spacing] = halo[("f", side * spacing)].astype(jnp.float32)
    branches = [features]
    for which, spacing in enumerate(dilations):
        total = jnp.zeros(features.shape, jnp.float32)
        for col_step in (-1, 0, 1):
            total = total + kernel[which, 4 + col_step][:, None, None] * jnp.roll(
                feat_rows[0], -col_step * spacing, axis=-1
            )
        total = lax.optimization_barrier(total)
        for row_step in (-1, 1):
            for col_step in (-1, 0, 1):
                tap_index = (row_step + 1) * 3 + col_step + 1
                total = total + kernel[which, tap_index][:, None, None] * jnp.roll(
                    feat_rows[row_step * spacing], -col_step * spacing, axis=-1
                )
        branches.append(total.astype(jnp.bfloat16))
    stacked = jnp.stack(branches)

    partial = jnp.einsum(
        "bchw,bco->ohw", stacked, pointwise, preferred_element_type=jnp.float32
    ).astype(jnp.bfloat16)
    result = lax.dynamic_slice_in_dim(partial, me * width, width, axis=0).astype(jnp.float32)
    for s in range(1, count):
        piece = lax.dynamic_slice_in_dim(partial, ((me + s) % count) * width, width, axis=0)
        result = result + chan_shift(piece, s).astype(jnp.float32)
    output = result.astype(jnp.bfloat16)

    point_local = jnp.zeros(pointwise.shape, jnp.float32)
    for s in range(count):
        point_slot = jnp.einsum(
            "bchw,ohw->bco", stacked, cot_full[s * width : (s + 1) * width],
            preferred_element_type=jnp.float32,
        )
        point_local = lax.dynamic_update_slice_in_dim(
            point_local, point_slot, ((me - s) % count) * width, axis=2
        )

    depth_rows = []
    for which, spacing in enumerate(dilations):
        grad_f = grad_branches[which + 1].astype(jnp.float32)
        tap_rows = []
        for tap_index in range(9):
            row_step = tap_index // 3 - 1
            col_step = tap_index % 3 - 1
            tap_rows.append(
                jnp.sum(
                    grad_f * jnp.roll(feat_rows[row_step * spacing], -col_step * spacing, axis=-1),
                    axis=(1, 2),
                )
            )
        depth_rows.append(jnp.stack(tap_rows))
    depth_local = jnp.stack(depth_rows)
    flat = jnp.concatenate([depth_local.reshape(-1), point_local.reshape(-1)])
    flat = band_allreduce(flat)
    depth_total = flat[: depth_local.size].reshape(depth_local.shape)
    point_total = flat[depth_local.size :].reshape(point_local.shape)

    grad_input = grad_branches[0].astype(jnp.float32)
    for which, spacing in enumerate(dilations):
        grad_f = grad_branches[which + 1].astype(jnp.float32)
        for col_step in (-1, 0, 1):
            grad_input = grad_input + kernel[which, 4 + col_step][:, None, None] * jnp.roll(
                grad_f, col_step * spacing, axis=-1
            )
    for which, spacing in enumerate(dilations):
        grad_input = lax.optimization_barrier(grad_input)
        for row_step in (-1, 1):
            rows = grad_halo[(which, -row_step * spacing)].astype(jnp.float32)
            for col_step in (-1, 0, 1):
                tap_index = (row_step + 1) * 3 + col_step + 1
                grad_input = grad_input + kernel[which, tap_index][:, None, None] * jnp.roll(
                    rows, col_step * spacing, axis=-1
                )
    return (output, grad_input, depth_total / GSCALE, point_total / GSCALE)


def solution(mesh):
    return jax.shard_map(
        block,
        mesh=mesh,
        in_specs=(
            P("chan", "band", None),
            P(None, None, "chan"),
            P(None, "chan", None),
            P("chan", "band", None),
        ),
        out_specs=(
            P("chan", "band", None),
            P("chan", "band", None),
            P(None, None, "chan"),
            P(None, "chan", None),
        ),
        check_vma=False,
    )
```

```python
import jax
import jax.numpy as jnp
from jax import lax
from jax.sharding import PartitionSpec as P


GSCALE = 1024


dilations = (6, 12, 18)


def shifted(block, axis, distance):
    devices = range(lax.axis_size(axis))
    route = [(i - distance, i) for i in devices if i - distance in devices]
    if not route:
        return jnp.zeros_like(block)
    return lax.ppermute(block, axis, route)


def pieces_of(height, offset):
    ahead, start = divmod(offset, height)
    if start == 0:
        return [(ahead, 0, height)]
    return [(ahead, start, height), (ahead + 1, 0, start)]


def halo_rows(requests):
    groups = {}
    for key, (field, offset) in requests.items():
        for ahead, first, last in pieces_of(field.shape[1], offset):
            groups.setdefault((ahead, last - first), []).append((key, field, first, last))
    got = {}
    for (ahead, rows), members in groups.items():
        blocks = [field[:, first:last] for _, field, first, last in members]
        joined = jnp.concatenate(blocks, axis=0) if len(blocks) > 1 else blocks[0]
        if ahead != 0:
            joined = shifted(joined, "band", -ahead)
        at = 0
        for (key, field, first, last), block in zip(members, blocks):
            got.setdefault(key, []).append((first, joined[at : at + block.shape[0]]))
            at += block.shape[0]
    out = {}
    for key, (field, offset) in requests.items():
        parts = got[key]
        out[key] = parts[0][1] if len(parts) == 1 else jnp.concatenate([p for _, p in parts], axis=1)
    return out


def band_allreduce(flat):
    count = lax.axis_size("band")
    radices = []
    rest = count
    while rest % 4 == 0:
        radices.append(4)
        rest //= 4
    while rest % 2 == 0:
        radices.append(2)
        rest //= 2
    if rest != 1:
        return lax.psum(flat, "band")
    length = flat.shape[0]
    flat = jnp.pad(flat, (0, (-length) % count))
    me = lax.axis_index("band")
    steps = []
    stride = 1
    for radix in radices:
        steps.append((stride, radix))
        stride *= radix

    def rotate(stride, radix, u):
        return [
            (j, j + (((j // stride) % radix + u) % radix - (j // stride) % radix) * stride)
            for j in range(count)
        ]

    for stride, radix in steps:
        digit = (me // stride) % radix
        size = flat.shape[0] // radix
        acc = lax.dynamic_slice_in_dim(flat, digit * size, size)
        for u in range(1, radix):
            give = lax.dynamic_slice_in_dim(flat, ((digit + u) % radix) * size, size)
            acc = acc + lax.ppermute(give, "band", rotate(stride, radix, u))
        flat = acc
    for stride, radix in reversed(steps):
        digit = (me // stride) % radix
        size = flat.shape[0]
        full = lax.dynamic_update_slice_in_dim(
            jnp.zeros((size * radix,), flat.dtype), flat, digit * size, 0
        )
        for u in range(1, radix):
            got = lax.ppermute(flat, "band", rotate(stride, radix, u))
            full = lax.dynamic_update_slice_in_dim(full, got, ((digit - u) % radix) * size, 0)
        flat = full
    return flat[:length]


def chan_shift(block, s):
    count = lax.axis_size("chan")
    return lax.ppermute(block, "chan", [(j, (j + s) % count) for j in range(count)])


def block(features, depth_kernel, pointwise, cotangent):
    kernel = depth_kernel.astype(jnp.float32)
    count = lax.axis_size("chan")
    width = pointwise.shape[2] // count
    cot_full = jnp.concatenate(
        [cotangent] + [chan_shift(cotangent, s) for s in range(1, count)], axis=0
    )
    requests = {}
    for spacing in dilations:
        for side in (-1, 1):
            requests[side * spacing] = (features, side * spacing)
    feat_halo = halo_rows(requests)
    me = lax.axis_index("chan")
    pw_slots = [
        lax.dynamic_slice_in_dim(pointwise, ((me - s) % count) * width, width, axis=2)
        for s in range(count)
    ]
    grad_sum = sum(
        jnp.einsum(
            "bco,ohw->bchw", pw_slots[s], cot_full[s * width : (s + 1) * width],
            preferred_element_type=jnp.float32,
        )
        for s in range(count)
    )
    grad_branches = grad_sum.astype(jnp.bfloat16)
    requests = {}
    for which, spacing in enumerate(dilations):
        for side in (-1, 1):
            requests[(which, side * spacing)] = (grad_branches[which + 1], side * spacing)
    grad_halo = halo_rows(requests)

    feat_rows = {0: features}
    feat_rows.update(feat_halo)
    branches = [features]
    for which, spacing in enumerate(dilations):
        total = jnp.zeros(features.shape, jnp.float32)
        for tap_index in range(9):
            row_step = tap_index // 3 - 1
            col_step = tap_index % 3 - 1
            total = total + kernel[which, tap_index][:, None, None] * jnp.roll(
                feat_rows[row_step * spacing], -col_step * spacing, axis=-1
            ).astype(jnp.float32)
        branches.append(total.astype(jnp.bfloat16))
    stacked = jnp.stack(branches)

    partial = jnp.einsum(
        "bchw,bco->ohw", stacked, pointwise, preferred_element_type=jnp.float32
    ).astype(jnp.bfloat16)
    result = lax.dynamic_slice_in_dim(partial, me * width, width, axis=0).astype(jnp.float32)
    for s in range(1, count):
        piece = lax.dynamic_slice_in_dim(partial, ((me + s) % count) * width, width, axis=0)
        result = result + chan_shift(piece, s).astype(jnp.float32)
    output = result.astype(jnp.bfloat16)

    point_local = jnp.zeros(pointwise.shape, jnp.float32)
    for s in range(count):
        point_slot = jnp.einsum(
            "bchw,ohw->bco", stacked, cot_full[s * width : (s + 1) * width],
            preferred_element_type=jnp.float32,
        )
        point_local = lax.dynamic_update_slice_in_dim(
            point_local, point_slot, ((me - s) % count) * width, axis=2
        )

    depth_rows = []
    for which, spacing in enumerate(dilations):
        grad_f = grad_branches[which + 1].astype(jnp.float32)
        tap_rows = []
        for tap_index in range(9):
            row_step = tap_index // 3 - 1
            col_step = tap_index % 3 - 1
            tap_rows.append(
                jnp.sum(
                    grad_f
                    * jnp.roll(feat_rows[row_step * spacing], -col_step * spacing, axis=-1).astype(
                        jnp.float32
                    ),
                    axis=(1, 2),
                )
            )
        depth_rows.append(jnp.stack(tap_rows))
    depth_local = jnp.stack(depth_rows)
    flat = jnp.concatenate([depth_local.reshape(-1), point_local.reshape(-1)])
    flat = band_allreduce(flat)
    depth_total = flat[: depth_local.size].reshape(depth_local.shape)
    point_total = flat[depth_local.size :].reshape(point_local.shape)

    grad_input = grad_branches[0].astype(jnp.float32)
    for which, spacing in enumerate(dilations):
        grad_f = grad_branches[which + 1].astype(jnp.float32)
        for col_step in (-1, 0, 1):
            grad_input = grad_input + kernel[which, 4 + col_step][:, None, None] * jnp.roll(
                grad_f, col_step * spacing, axis=-1
            )
    for which, spacing in enumerate(dilations):
        grad_input = lax.optimization_barrier(grad_input)
        for row_step in (-1, 1):
            rows = grad_halo[(which, -row_step * spacing)]
            for col_step in (-1, 0, 1):
                tap_index = (row_step + 1) * 3 + col_step + 1
                grad_input = grad_input + kernel[which, tap_index][:, None, None] * jnp.roll(
                    rows, col_step * spacing, axis=-1
                ).astype(jnp.float32)
    return (output, grad_input, depth_total / GSCALE, point_total / GSCALE)


def solution(mesh):
    return jax.shard_map(
        block,
        mesh=mesh,
        in_specs=(
            P("chan", "band", None),
            P(None, None, "chan"),
            P(None, "chan", None),
            P("chan", "band", None),
        ),
        out_specs=(
            P("chan", "band", None),
            P("chan", "band", None),
            P(None, None, "chan"),
            P(None, "chan", None),
        ),
        check_vma=False,
    )
```

```python
import jax
import jax.numpy as jnp
from jax import lax
from jax.sharding import PartitionSpec as P


GSCALE = 1024


dilations = (6, 12, 18)


def shifted(block, axis, distance):
    devices = range(lax.axis_size(axis))
    route = [(i - distance, i) for i in devices if i - distance in devices]
    if not route:
        return jnp.zeros_like(block)
    return lax.ppermute(block, axis, route)


def pieces_of(height, offset):
    ahead, start = divmod(offset, height)
    if start == 0:
        return [(ahead, 0, height)]
    return [(ahead, start, height), (ahead + 1, 0, start)]


def halo_rows(requests):
    groups = {}
    for key, (field, offset) in requests.items():
        for ahead, first, last in pieces_of(field.shape[1], offset):
            groups.setdefault((ahead, last - first), []).append((key, field, first, last))
    got = {}
    for (ahead, rows), members in groups.items():
        blocks = [field[:, first:last] for _, field, first, last in members]
        joined = jnp.concatenate(blocks, axis=0) if len(blocks) > 1 else blocks[0]
        if ahead != 0:
            joined = shifted(joined, "band", -ahead)
        at = 0
        for (key, field, first, last), block in zip(members, blocks):
            got.setdefault(key, []).append((first, joined[at : at + block.shape[0]]))
            at += block.shape[0]
    out = {}
    for key, (field, offset) in requests.items():
        parts = got[key]
        out[key] = parts[0][1] if len(parts) == 1 else jnp.concatenate([p for _, p in parts], axis=1)
    return out


def band_allreduce(flat):
    count = lax.axis_size("band")
    radices = []
    rest = count
    while rest % 2 == 0:
        radices.append(2)
        rest //= 2
    if rest != 1:
        return lax.psum(flat, "band")
    length = flat.shape[0]
    flat = jnp.pad(flat, (0, (-length) % count))
    me = lax.axis_index("band")
    steps = []
    stride = 1
    for radix in radices:
        steps.append((stride, radix))
        stride *= radix

    def rotate(stride, radix, u):
        return [
            (j, j + (((j // stride) % radix + u) % radix - (j // stride) % radix) * stride)
            for j in range(count)
        ]

    for stride, radix in steps:
        digit = (me // stride) % radix
        size = flat.shape[0] // radix
        acc = lax.dynamic_slice_in_dim(flat, digit * size, size)
        for u in range(1, radix):
            give = lax.dynamic_slice_in_dim(flat, ((digit + u) % radix) * size, size)
            acc = acc + lax.ppermute(give, "band", rotate(stride, radix, u))
        flat = acc
    for stride, radix in reversed(steps):
        digit = (me // stride) % radix
        size = flat.shape[0]
        full = lax.dynamic_update_slice_in_dim(
            jnp.zeros((size * radix,), flat.dtype), flat, digit * size, 0
        )
        for u in range(1, radix):
            got = lax.ppermute(flat, "band", rotate(stride, radix, u))
            full = lax.dynamic_update_slice_in_dim(full, got, ((digit - u) % radix) * size, 0)
        flat = full
    return flat[:length]


def chan_shift(block, s):
    count = lax.axis_size("chan")
    return lax.ppermute(block, "chan", [(j, (j + s) % count) for j in range(count)])


def block(features, depth_kernel, pointwise, cotangent):
    kernel = depth_kernel.astype(jnp.float32)
    count = lax.axis_size("chan")
    width = pointwise.shape[2] // count
    cot_full = jnp.concatenate(
        [cotangent] + [chan_shift(cotangent, s) for s in range(1, count)], axis=0
    )
    requests = {}
    for spacing in dilations:
        for side in (-1, 1):
            requests[side * spacing] = (features, side * spacing)
    feat_halo = halo_rows(requests)
    me = lax.axis_index("chan")
    pw_slots = [
        lax.dynamic_slice_in_dim(pointwise, ((me - s) % count) * width, width, axis=2)
        for s in range(count)
    ]
    grad_sum = sum(
        jnp.einsum(
            "bco,ohw->bchw", pw_slots[s], cot_full[s * width : (s + 1) * width],
            preferred_element_type=jnp.float32,
        )
        for s in range(count)
    )
    grad_branches = grad_sum.astype(jnp.bfloat16)
    requests = {}
    for which, spacing in enumerate(dilations):
        for side in (-1, 1):
            requests[(which, side * spacing)] = (grad_branches[which + 1], side * spacing)
    grad_halo = halo_rows(requests)

    feat_rows = {0: features.astype(jnp.float32)}
    for offset, rows in feat_halo.items():
        feat_rows[offset] = rows.astype(jnp.float32)
    branches = [features]
    for which, spacing in enumerate(dilations):
        total = jnp.zeros(features.shape, jnp.float32)
        for tap_index in range(9):
            row_step = tap_index // 3 - 1
            col_step = tap_index % 3 - 1
            total = total + kernel[which, tap_index][:, None, None] * jnp.roll(
                feat_rows[row_step * spacing], -col_step * spacing, axis=-1
            )
        branches.append(total.astype(jnp.bfloat16))
    stacked = jnp.stack(branches)

    partial = jnp.einsum(
        "bchw,bco->ohw", stacked, pointwise, preferred_element_type=jnp.float32
    ).astype(jnp.bfloat16)
    result = lax.dynamic_slice_in_dim(partial, me * width, width, axis=0).astype(jnp.float32)
    for s in range(1, count):
        piece = lax.dynamic_slice_in_dim(partial, ((me + s) % count) * width, width, axis=0)
        result = result + chan_shift(piece, s).astype(jnp.float32)
    output = result.astype(jnp.bfloat16)

    point_local = jnp.zeros(pointwise.shape, jnp.float32)
    for s in range(count):
        point_slot = jnp.einsum(
            "bchw,ohw->bco", stacked, cot_full[s * width : (s + 1) * width],
            preferred_element_type=jnp.float32,
        )
        point_local = lax.dynamic_update_slice_in_dim(
            point_local, point_slot, ((me - s) % count) * width, axis=2
        )

    depth_rows = []
    for which, spacing in enumerate(dilations):
        grad_f = grad_branches[which + 1].astype(jnp.float32)
        tap_rows = []
        for tap_index in range(9):
            row_step = tap_index // 3 - 1
            col_step = tap_index % 3 - 1
            tap_rows.append(
                jnp.sum(
                    grad_f * jnp.roll(feat_rows[row_step * spacing], -col_step * spacing, axis=-1),
                    axis=(1, 2),
                )
            )
        depth_rows.append(jnp.stack(tap_rows))
    depth_local = jnp.stack(depth_rows)
    flat = jnp.concatenate([depth_local.reshape(-1), point_local.reshape(-1)])
    flat = band_allreduce(flat)
    depth_total = flat[: depth_local.size].reshape(depth_local.shape)
    point_total = flat[depth_local.size :].reshape(point_local.shape)

    grad_input = grad_branches[0].astype(jnp.float32)
    for which, spacing in enumerate(dilations):
        grad_f = grad_branches[which + 1].astype(jnp.float32)
        for col_step in (-1, 0, 1):
            grad_input = grad_input + kernel[which, 4 + col_step][:, None, None] * jnp.roll(
                grad_f, col_step * spacing, axis=-1
            )
    for which, spacing in enumerate(dilations):
        grad_input = lax.optimization_barrier(grad_input)
        for row_step in (-1, 1):
            rows = grad_halo[(which, -row_step * spacing)].astype(jnp.float32)
            for col_step in (-1, 0, 1):
                tap_index = (row_step + 1) * 3 + col_step + 1
                grad_input = grad_input + kernel[which, tap_index][:, None, None] * jnp.roll(
                    rows, col_step * spacing, axis=-1
                )
    return (output, grad_input, depth_total / GSCALE, point_total / GSCALE)


def solution(mesh):
    return jax.shard_map(
        block,
        mesh=mesh,
        in_specs=(
            P("chan", "band", None),
            P(None, None, "chan"),
            P(None, "chan", None),
            P("chan", "band", None),
        ),
        out_specs=(
            P("chan", "band", None),
            P("chan", "band", None),
            P(None, None, "chan"),
            P(None, "chan", None),
        ),
        check_vma=False,
    )
```

```python
import jax
import jax.numpy as jnp
from jax import lax
from jax.sharding import PartitionSpec as P


GSCALE = 1024


dilations = (6, 12, 18)


def shifted(block, axis, distance):
    devices = range(lax.axis_size(axis))
    route = [(i - distance, i) for i in devices if i - distance in devices]
    if not route:
        return jnp.zeros_like(block)
    return lax.ppermute(block, axis, route)


def pieces_of(height, offset):
    ahead, start = divmod(offset, height)
    if start == 0:
        return [(ahead, 0, height)]
    return [(ahead, start, height), (ahead + 1, 0, start)]


def halo_rows(requests):
    groups = {}
    for key, (field, offset) in requests.items():
        for ahead, first, last in pieces_of(field.shape[1], offset):
            groups.setdefault((ahead, last - first), []).append((key, field, first, last))
    got = {}
    for (ahead, rows), members in groups.items():
        blocks = [field[:, first:last] for _, field, first, last in members]
        joined = jnp.concatenate(blocks, axis=0) if len(blocks) > 1 else blocks[0]
        if ahead != 0:
            joined = shifted(joined, "band", -ahead)
        at = 0
        for (key, field, first, last), block in zip(members, blocks):
            got.setdefault(key, []).append((first, joined[at : at + block.shape[0]]))
            at += block.shape[0]
    out = {}
    for key, (field, offset) in requests.items():
        parts = got[key]
        out[key] = parts[0][1] if len(parts) == 1 else jnp.concatenate([p for _, p in parts], axis=1)
    return out


def band_allreduce(flat):
    count = lax.axis_size("band")
    radices = []
    rest = count
    while rest % 4 == 0:
        radices.append(4)
        rest //= 4
    while rest % 2 == 0:
        radices.append(2)
        rest //= 2
    if rest != 1:
        return lax.psum(flat, "band")
    length = flat.shape[0]
    flat = jnp.pad(flat, (0, (-length) % count))
    me = lax.axis_index("band")
    steps = []
    stride = 1
    for radix in radices:
        steps.append((stride, radix))
        stride *= radix

    def rotate(stride, radix, u):
        return [
            (j, j + (((j // stride) % radix + u) % radix - (j // stride) % radix) * stride)
            for j in range(count)
        ]

    for stride, radix in steps:
        digit = (me // stride) % radix
        size = flat.shape[0] // radix
        acc = lax.dynamic_slice_in_dim(flat, digit * size, size)
        for u in range(1, radix):
            give = lax.dynamic_slice_in_dim(flat, ((digit + u) % radix) * size, size)
            acc = acc + lax.ppermute(give, "band", rotate(stride, radix, u))
        flat = acc
    for stride, radix in reversed(steps):
        digit = (me // stride) % radix
        size = flat.shape[0]
        full = lax.dynamic_update_slice_in_dim(
            jnp.zeros((size * radix,), flat.dtype), flat, digit * size, 0
        )
        for u in range(1, radix):
            got = lax.ppermute(flat, "band", rotate(stride, radix, u))
            full = lax.dynamic_update_slice_in_dim(full, got, ((digit - u) % radix) * size, 0)
        flat = full
    return flat[:length]


def chan_shift(block, s):
    count = lax.axis_size("chan")
    return lax.ppermute(block, "chan", [(j, (j + s) % count) for j in range(count)])


def block(features, depth_kernel, pointwise, cotangent):
    kernel = depth_kernel.astype(jnp.float32)
    count = lax.axis_size("chan")
    width = pointwise.shape[2] // count
    me = lax.axis_index("chan")
    slots = jnp.stack([cotangent] + [chan_shift(cotangent, s) for s in range(1, count)])
    cot_full = jnp.take(slots, (me - jnp.arange(count)) % count, axis=0).reshape(
        (count * cotangent.shape[0],) + cotangent.shape[1:]
    )
    requests = {}
    for spacing in dilations:
        for side in (-1, 1):
            requests[side * spacing] = (features, side * spacing)
    feat_halo = halo_rows(requests)
    grad_sum = jnp.einsum("bco,ohw->bchw", pointwise, cot_full, preferred_element_type=jnp.float32)
    grad_branches = grad_sum.astype(jnp.bfloat16)
    requests = {}
    for which, spacing in enumerate(dilations):
        for side in (-1, 1):
            requests[(which, side * spacing)] = (grad_branches[which + 1], side * spacing)
    grad_halo = halo_rows(requests)

    feat_rows = {0: features.astype(jnp.float32)}
    for offset, rows in feat_halo.items():
        feat_rows[offset] = rows.astype(jnp.float32)
    branches = [features]
    for which, spacing in enumerate(dilations):
        total = jnp.zeros(features.shape, jnp.float32)
        for tap_index in range(9):
            row_step = tap_index // 3 - 1
            col_step = tap_index % 3 - 1
            total = total + kernel[which, tap_index][:, None, None] * jnp.roll(
                feat_rows[row_step * spacing], -col_step * spacing, axis=-1
            )
        branches.append(total.astype(jnp.bfloat16))
    stacked = jnp.stack(branches)

    partial = jnp.einsum(
        "bchw,bco->ohw", stacked, pointwise, preferred_element_type=jnp.float32
    ).astype(jnp.bfloat16)
    result = lax.dynamic_slice_in_dim(partial, me * width, width, axis=0).astype(jnp.float32)
    for s in range(1, count):
        piece = lax.dynamic_slice_in_dim(partial, ((me + s) % count) * width, width, axis=0)
        result = result + chan_shift(piece, s).astype(jnp.float32)
    output = result.astype(jnp.bfloat16)

    point_local = jnp.einsum("bchw,ohw->bco", stacked, cot_full, preferred_element_type=jnp.float32)

    depth_rows = []
    for which, spacing in enumerate(dilations):
        grad_f = grad_branches[which + 1].astype(jnp.float32)
        tap_rows = []
        for tap_index in range(9):
            row_step = tap_index // 3 - 1
            col_step = tap_index % 3 - 1
            tap_rows.append(
                jnp.sum(
                    grad_f * jnp.roll(feat_rows[row_step * spacing], -col_step * spacing, axis=-1),
                    axis=(1, 2),
                )
            )
        depth_rows.append(jnp.stack(tap_rows))
    depth_local = jnp.stack(depth_rows)
    flat = jnp.concatenate([depth_local.reshape(-1), point_local.reshape(-1)])
    flat = band_allreduce(flat)
    depth_total = flat[: depth_local.size].reshape(depth_local.shape)
    point_total = flat[depth_local.size :].reshape(point_local.shape)

    grad_input = grad_branches[0].astype(jnp.float32)
    for which, spacing in enumerate(dilations):
        grad_f = grad_branches[which + 1].astype(jnp.float32)
        for col_step in (-1, 0, 1):
            grad_input = grad_input + kernel[which, 4 + col_step][:, None, None] * jnp.roll(
                grad_f, col_step * spacing, axis=-1
            )
    for which, spacing in enumerate(dilations):
        grad_input = lax.optimization_barrier(grad_input)
        for row_step in (-1, 1):
            rows = grad_halo[(which, -row_step * spacing)].astype(jnp.float32)
            for col_step in (-1, 0, 1):
                tap_index = (row_step + 1) * 3 + col_step + 1
                grad_input = grad_input + kernel[which, tap_index][:, None, None] * jnp.roll(
                    rows, col_step * spacing, axis=-1
                )
    return (output, grad_input, depth_total / GSCALE, point_total / GSCALE)


def solution(mesh):
    return jax.shard_map(
        block,
        mesh=mesh,
        in_specs=(
            P("chan", "band", None),
            P(None, None, "chan"),
            P(None, "chan", None),
            P("chan", "band", None),
        ),
        out_specs=(
            P("chan", "band", None),
            P("chan", "band", None),
            P(None, None, "chan"),
            P(None, "chan", None),
        ),
        check_vma=False,
    )
```

```python
import jax
import jax.numpy as jnp
from jax import lax
from jax.sharding import PartitionSpec as P


GSCALE = 1024


dilations = (6, 12, 18)


def shifted(block, axis, distance):
    devices = range(lax.axis_size(axis))
    route = [(i - distance, i) for i in devices if i - distance in devices]
    if not route:
        return jnp.zeros_like(block)
    return lax.ppermute(block, axis, route)


def pieces_of(height, offset):
    ahead, start = divmod(offset, height)
    if start == 0:
        return [(ahead, 0, height)]
    return [(ahead, start, height), (ahead + 1, 0, start)]


def halo_rows(requests):
    groups = {}
    for key, (field, offset) in requests.items():
        for ahead, first, last in pieces_of(field.shape[1], offset):
            groups.setdefault((ahead, last - first), []).append((key, field, first, last))
    got = {}
    for (ahead, rows), members in groups.items():
        blocks = [field[:, first:last] for _, field, first, last in members]
        joined = jnp.concatenate(blocks, axis=0) if len(blocks) > 1 else blocks[0]
        if ahead != 0:
            joined = shifted(joined, "band", -ahead)
        at = 0
        for (key, field, first, last), block in zip(members, blocks):
            got.setdefault(key, []).append((first, joined[at : at + block.shape[0]]))
            at += block.shape[0]
    out = {}
    for key, (field, offset) in requests.items():
        parts = got[key]
        out[key] = parts[0][1] if len(parts) == 1 else jnp.concatenate([p for _, p in parts], axis=1)
    return out


def band_allreduce(flat):
    count = lax.axis_size("band")
    radices = []
    rest = count
    while rest % 4 == 0:
        radices.append(4)
        rest //= 4
    while rest % 2 == 0:
        radices.append(2)
        rest //= 2
    if rest != 1:
        return lax.psum(flat, "band")
    length = flat.shape[0]
    flat = jnp.pad(flat, (0, (-length) % count))
    me = lax.axis_index("band")
    steps = []
    stride = 1
    for radix in radices:
        steps.append((stride, radix))
        stride *= radix

    def rotate(stride, radix, u):
        return [
            (j, j + (((j // stride) % radix + u) % radix - (j // stride) % radix) * stride)
            for j in range(count)
        ]

    for stride, radix in steps:
        digit = (me // stride) % radix
        size = flat.shape[0] // radix
        acc = lax.dynamic_slice_in_dim(flat, digit * size, size)
        for u in range(1, radix):
            give = lax.dynamic_slice_in_dim(flat, ((digit + u) % radix) * size, size)
            acc = acc + lax.ppermute(give, "band", rotate(stride, radix, u))
        flat = acc
    for stride, radix in reversed(steps):
        digit = (me // stride) % radix
        size = flat.shape[0]
        full = lax.dynamic_update_slice_in_dim(
            jnp.zeros((size * radix,), flat.dtype), flat, digit * size, 0
        )
        for u in range(1, radix):
            got = lax.ppermute(flat, "band", rotate(stride, radix, u))
            full = lax.dynamic_update_slice_in_dim(full, got, ((digit - u) % radix) * size, 0)
        flat = full
    return flat[:length]


def chan_shift(block, s):
    count = lax.axis_size("chan")
    return lax.ppermute(block, "chan", [(j, (j + s) % count) for j in range(count)])


def block(features, depth_kernel, pointwise, cotangent):
    kernel = depth_kernel.astype(jnp.float32)
    count = lax.axis_size("chan")
    width = pointwise.shape[2] // count
    cot_full = jnp.concatenate(
        [cotangent] + [chan_shift(cotangent, s) for s in range(1, count)], axis=0
    )
    requests = {}
    for spacing in dilations:
        for side in (-1, 1):
            requests[side * spacing] = (features, side * spacing)
    feat_halo = halo_rows(requests)
    me = lax.axis_index("chan")
    pw_slots = [
        lax.dynamic_slice_in_dim(pointwise, ((me - s) % count) * width, width, axis=2)
        for s in range(count)
    ]
    grad_sum = sum(
        jnp.einsum(
            "bco,ohw->bchw", pw_slots[s], cot_full[s * width : (s + 1) * width],
            preferred_element_type=jnp.float32,
        )
        for s in range(count)
    )
    grad_branches = grad_sum.astype(jnp.bfloat16)
    requests = {}
    for which, spacing in enumerate(dilations):
        for side in (-1, 1):
            requests[(which, side * spacing)] = (grad_branches[which + 1], side * spacing)
    grad_halo = halo_rows(requests)

    feat_rows = {0: features.astype(jnp.float32)}
    for offset, rows in feat_halo.items():
        feat_rows[offset] = rows.astype(jnp.float32)
    branches = [features]
    for which, spacing in enumerate(dilations):
        total = jnp.zeros(features.shape, jnp.float32)
        for tap_index in range(9):
            row_step = tap_index // 3 - 1
            col_step = tap_index % 3 - 1
            total = total + kernel[which, tap_index][:, None, None] * jnp.roll(
                feat_rows[row_step * spacing], -col_step * spacing, axis=-1
            )
        branches.append(total.astype(jnp.bfloat16))
    stacked = jnp.stack(branches)

    partial = jnp.einsum(
        "bchw,bco->ohw", stacked, pointwise, preferred_element_type=jnp.float32
    ).astype(jnp.bfloat16)
    result = lax.dynamic_slice_in_dim(partial, me * width, width, axis=0).astype(jnp.float32)
    for s in range(1, count):
        piece = lax.dynamic_slice_in_dim(partial, ((me + s) % count) * width, width, axis=0)
        result = result + chan_shift(piece, s).astype(jnp.float32)
    output = result.astype(jnp.bfloat16)

    point_local = jnp.zeros(pointwise.shape, jnp.float32)
    for s in range(count):
        point_slot = jnp.einsum(
            "bchw,ohw->bco", stacked, cot_full[s * width : (s + 1) * width],
            preferred_element_type=jnp.float32,
        )
        point_local = lax.dynamic_update_slice_in_dim(
            point_local, point_slot, ((me - s) % count) * width, axis=2
        )

    depth_rows = []
    for which, spacing in enumerate(dilations):
        grad_f = grad_branches[which + 1].astype(jnp.float32)
        tap_rows = []
        for tap_index in range(9):
            row_step = tap_index // 3 - 1
            col_step = tap_index % 3 - 1
            tap_rows.append(
                jnp.sum(
                    grad_f * jnp.roll(feat_rows[row_step * spacing], -col_step * spacing, axis=-1),
                    axis=(1, 2),
                )
            )
        depth_rows.append(jnp.stack(tap_rows))
    depth_local = jnp.stack(depth_rows)
    flat = jnp.concatenate([depth_local.reshape(-1), point_local.reshape(-1)])
    flat = band_allreduce(flat)
    depth_total = flat[: depth_local.size].reshape(depth_local.shape)
    point_total = flat[depth_local.size :].reshape(point_local.shape)

    grad_input = grad_branches[0].astype(jnp.float32)
    for which, spacing in enumerate(dilations):
        grad_f = grad_branches[which + 1].astype(jnp.float32)
        for col_step in (-1, 0, 1):
            grad_input = grad_input + kernel[which, 4 + col_step][:, None, None] * jnp.roll(
                grad_f, col_step * spacing, axis=-1
            )
    for which, spacing in enumerate(dilations):
        grad_input = lax.optimization_barrier(grad_input)
        for row_step in (-1, 1):
            rows = grad_halo[(which, -row_step * spacing)]
            for col_step in (-1, 0, 1):
                tap_index = (row_step + 1) * 3 + col_step + 1
                grad_input = grad_input + kernel[which, tap_index][:, None, None] * jnp.roll(
                    rows, col_step * spacing, axis=-1
                ).astype(jnp.float32)
    return (output, grad_input, depth_total / GSCALE, point_total / GSCALE)


def solution(mesh):
    return jax.shard_map(
        block,
        mesh=mesh,
        in_specs=(
            P("chan", "band", None),
            P(None, None, "chan"),
            P(None, "chan", None),
            P("chan", "band", None),
        ),
        out_specs=(
            P("chan", "band", None),
            P("chan", "band", None),
            P(None, None, "chan"),
            P(None, "chan", None),
        ),
        check_vma=False,
    )
```

```python
import jax
import jax.numpy as jnp
from jax import lax
from jax.sharding import PartitionSpec as P


GSCALE = 1024


dilations = (6, 12, 18)


def shifted(block, axis, distance):
    devices = range(lax.axis_size(axis))
    route = [(i - distance, i) for i in devices if i - distance in devices]
    if not route:
        return jnp.zeros_like(block)
    return lax.ppermute(block, axis, route)


def pieces_of(height, offset):
    ahead, start = divmod(offset, height)
    if start == 0:
        return [(ahead, 0, height)]
    return [(ahead, start, height), (ahead + 1, 0, start)]


def halo_rows(requests):
    groups = {}
    for key, (field, offset) in requests.items():
        for ahead, first, last in pieces_of(field.shape[1], offset):
            groups.setdefault((ahead, last - first), []).append((key, field, first, last))
    got = {}
    for (ahead, rows), members in groups.items():
        blocks = [field[:, first:last] for _, field, first, last in members]
        joined = jnp.concatenate(blocks, axis=0) if len(blocks) > 1 else blocks[0]
        if ahead != 0:
            joined = shifted(joined, "band", -ahead)
        at = 0
        for (key, field, first, last), block in zip(members, blocks):
            got.setdefault(key, []).append((first, joined[at : at + block.shape[0]]))
            at += block.shape[0]
    out = {}
    for key, (field, offset) in requests.items():
        parts = got[key]
        out[key] = parts[0][1] if len(parts) == 1 else jnp.concatenate([p for _, p in parts], axis=1)
    return out


def band_allreduce(flat):
    count = lax.axis_size("band")
    radices = []
    rest = count
    while rest % 4 == 0:
        radices.append(4)
        rest //= 4
    while rest % 2 == 0:
        radices.append(2)
        rest //= 2
    if rest != 1:
        return lax.psum(flat, "band")
    length = flat.shape[0]
    flat = jnp.pad(flat, (0, (-length) % count))
    me = lax.axis_index("band")
    steps = []
    stride = 1
    for radix in radices:
        steps.append((stride, radix))
        stride *= radix

    def rotate(stride, radix, u):
        return [
            (j, j + (((j // stride) % radix + u) % radix - (j // stride) % radix) * stride)
            for j in range(count)
        ]

    for stride, radix in steps:
        digit = (me // stride) % radix
        size = flat.shape[0] // radix
        acc = lax.dynamic_slice_in_dim(flat, digit * size, size)
        for u in range(1, radix):
            give = lax.dynamic_slice_in_dim(flat, ((digit + u) % radix) * size, size)
            acc = acc + lax.ppermute(give, "band", rotate(stride, radix, u))
        flat = acc
    for stride, radix in reversed(steps):
        digit = (me // stride) % radix
        size = flat.shape[0]
        full = lax.dynamic_update_slice_in_dim(
            jnp.zeros((size * radix,), flat.dtype), flat, digit * size, 0
        )
        for u in range(1, radix):
            got = lax.ppermute(flat, "band", rotate(stride, radix, u))
            full = lax.dynamic_update_slice_in_dim(full, got, ((digit - u) % radix) * size, 0)
        flat = full
    return flat[:length]


def chan_shift(block, s):
    count = lax.axis_size("chan")
    return lax.ppermute(block, "chan", [(j, (j + s) % count) for j in range(count)])


def block(features, depth_kernel, pointwise, cotangent):
    kernel = depth_kernel.astype(jnp.float32)
    count = lax.axis_size("chan")
    width = pointwise.shape[2] // count
    cot_full = jnp.concatenate(
        [cotangent] + [chan_shift(cotangent, s) for s in range(1, count)], axis=0
    )
    requests = {}
    for spacing in dilations:
        for side in (-1, 1):
            requests[side * spacing] = (features, side * spacing)
    feat_halo = halo_rows(requests)
    me = lax.axis_index("chan")
    pw_slots = [
        lax.dynamic_slice_in_dim(pointwise, ((me - s) % count) * width, width, axis=2)
        for s in range(count)
    ]
    grad_sum = sum(
        jnp.einsum(
            "bco,ohw->bchw", pw_slots[s], cot_full[s * width : (s + 1) * width],
            preferred_element_type=jnp.float32,
        )
        for s in range(count)
    )
    grad_branches = grad_sum.astype(jnp.bfloat16)
    requests = {}
    for which, spacing in enumerate(dilations):
        for side in (-1, 1):
            requests[(which, side * spacing)] = (grad_branches[which + 1], side * spacing)
    grad_halo = halo_rows(requests)

    feat_rows = {0: features.astype(jnp.float32)}
    for offset, rows in feat_halo.items():
        feat_rows[offset] = rows.astype(jnp.float32)
    centres = []
    for which, spacing in enumerate(dilations):
        total = jnp.zeros(features.shape, jnp.float32)
        for col_step in (-1, 0, 1):
            total = total + kernel[which, 4 + col_step][:, None, None] * jnp.roll(
                feat_rows[0], -col_step * spacing, axis=-1
            )
        centres.append(lax.optimization_barrier(total))
    branches = [features]
    for which, spacing in enumerate(dilations):
        total = centres[which]
        for row_step in (-1, 1):
            for col_step in (-1, 0, 1):
                tap_index = (row_step + 1) * 3 + col_step + 1
                total = total + kernel[which, tap_index][:, None, None] * jnp.roll(
                    feat_rows[row_step * spacing], -col_step * spacing, axis=-1
                )
        branches.append(total.astype(jnp.bfloat16))
    stacked = jnp.stack(branches)

    partial = jnp.einsum(
        "bchw,bco->ohw", stacked, pointwise, preferred_element_type=jnp.float32
    ).astype(jnp.bfloat16)
    result = lax.dynamic_slice_in_dim(partial, me * width, width, axis=0).astype(jnp.float32)
    for s in range(1, count):
        piece = lax.dynamic_slice_in_dim(partial, ((me + s) % count) * width, width, axis=0)
        result = result + chan_shift(piece, s).astype(jnp.float32)
    output = result.astype(jnp.bfloat16)

    point_local = jnp.zeros(pointwise.shape, jnp.float32)
    for s in range(count):
        point_slot = jnp.einsum(
            "bchw,ohw->bco", stacked, cot_full[s * width : (s + 1) * width],
            preferred_element_type=jnp.float32,
        )
        point_local = lax.dynamic_update_slice_in_dim(
            point_local, point_slot, ((me - s) % count) * width, axis=2
        )

    depth_rows = []
    for which, spacing in enumerate(dilations):
        grad_f = grad_branches[which + 1].astype(jnp.float32)
        tap_rows = []
        for tap_index in range(9):
            row_step = tap_index // 3 - 1
            col_step = tap_index % 3 - 1
            tap_rows.append(
                jnp.sum(
                    grad_f * jnp.roll(feat_rows[row_step * spacing], -col_step * spacing, axis=-1),
                    axis=(1, 2),
                )
            )
        depth_rows.append(jnp.stack(tap_rows))
    depth_local = jnp.stack(depth_rows)
    flat = jnp.concatenate([depth_local.reshape(-1), point_local.reshape(-1)])
    flat = band_allreduce(flat)
    depth_total = flat[: depth_local.size].reshape(depth_local.shape)
    point_total = flat[depth_local.size :].reshape(point_local.shape)

    grad_input = grad_branches[0].astype(jnp.float32)
    for which, spacing in enumerate(dilations):
        grad_f = grad_branches[which + 1].astype(jnp.float32)
        for col_step in (-1, 0, 1):
            grad_input = grad_input + kernel[which, 4 + col_step][:, None, None] * jnp.roll(
                grad_f, col_step * spacing, axis=-1
            )
    for which, spacing in enumerate(dilations):
        grad_input = lax.optimization_barrier(grad_input)
        for row_step in (-1, 1):
            rows = grad_halo[(which, -row_step * spacing)].astype(jnp.float32)
            for col_step in (-1, 0, 1):
                tap_index = (row_step + 1) * 3 + col_step + 1
                grad_input = grad_input + kernel[which, tap_index][:, None, None] * jnp.roll(
                    rows, col_step * spacing, axis=-1
                )
    return (output, grad_input, depth_total / GSCALE, point_total / GSCALE)


def solution(mesh):
    return jax.shard_map(
        block,
        mesh=mesh,
        in_specs=(
            P("chan", "band", None),
            P(None, None, "chan"),
            P(None, "chan", None),
            P("chan", "band", None),
        ),
        out_specs=(
            P("chan", "band", None),
            P("chan", "band", None),
            P(None, None, "chan"),
            P(None, "chan", None),
        ),
        check_vma=False,
    )
```

```python
import jax
import jax.numpy as jnp
from jax import lax
from jax.sharding import PartitionSpec as P


GSCALE = 1024


dilations = (6, 12, 18)


def shifted(block, axis, distance):
    devices = range(lax.axis_size(axis))
    route = [(i - distance, i) for i in devices if i - distance in devices]
    if not route:
        return jnp.zeros_like(block)
    return lax.ppermute(block, axis, route)


def pieces_of(height, offset):
    ahead, start = divmod(offset, height)
    if start == 0:
        return [(ahead, 0, height)]
    return [(ahead, start, height), (ahead + 1, 0, start)]


def halo_rows(requests):
    groups = {}
    for key, (field, offset) in requests.items():
        for ahead, first, last in pieces_of(field.shape[1], offset):
            groups.setdefault((ahead, last - first), []).append((key, field, first, last))
    got = {}
    for (ahead, rows), members in groups.items():
        blocks = [field[:, first:last] for _, field, first, last in members]
        joined = jnp.concatenate(blocks, axis=0) if len(blocks) > 1 else blocks[0]
        if ahead != 0:
            joined = shifted(joined, "band", -ahead)
        at = 0
        for (key, field, first, last), block in zip(members, blocks):
            got.setdefault(key, []).append((first, joined[at : at + block.shape[0]]))
            at += block.shape[0]
    out = {}
    for key, (field, offset) in requests.items():
        parts = got[key]
        out[key] = parts[0][1] if len(parts) == 1 else jnp.concatenate([p for _, p in parts], axis=1)
    return out


def band_allreduce(flat):
    count = lax.axis_size("band")
    radices = []
    rest = count
    while rest % 4 == 0:
        radices.append(4)
        rest //= 4
    while rest % 2 == 0:
        radices.append(2)
        rest //= 2
    if rest != 1:
        return lax.psum(flat, "band")
    length = flat.shape[0]
    flat = jnp.pad(flat, (0, (-length) % count))
    me = lax.axis_index("band")
    steps = []
    stride = 1
    for radix in radices:
        steps.append((stride, radix))
        stride *= radix

    def rotate(stride, radix, u):
        return [
            (j, j + (((j // stride) % radix + u) % radix - (j // stride) % radix) * stride)
            for j in range(count)
        ]

    for stride, radix in steps:
        digit = (me // stride) % radix
        size = flat.shape[0] // radix
        acc = lax.dynamic_slice_in_dim(flat, digit * size, size)
        for u in range(1, radix):
            give = lax.dynamic_slice_in_dim(flat, ((digit + u) % radix) * size, size)
            acc = acc + lax.ppermute(give, "band", rotate(stride, radix, u))
        flat = acc
    for stride, radix in reversed(steps):
        digit = (me // stride) % radix
        size = flat.shape[0]
        full = lax.dynamic_update_slice_in_dim(
            jnp.zeros((size * radix,), flat.dtype), flat, digit * size, 0
        )
        for u in range(1, radix):
            got = lax.ppermute(flat, "band", rotate(stride, radix, u))
            full = lax.dynamic_update_slice_in_dim(full, got, ((digit - u) % radix) * size, 0)
        flat = full
    return flat[:length]


def chan_shift(block, s):
    count = lax.axis_size("chan")
    return lax.ppermute(block, "chan", [(j, (j + s) % count) for j in range(count)])


def block(features, depth_kernel, pointwise, cotangent):
    kernel = depth_kernel.astype(jnp.float32)
    count = lax.axis_size("chan")
    width = pointwise.shape[2] // count
    cot_full = jnp.concatenate(
        [cotangent] + [chan_shift(cotangent, s) for s in range(1, count)], axis=0
    )
    requests = {}
    for spacing in dilations:
        for side in (-1, 1):
            requests[side * spacing] = (features, side * spacing)
    feat_halo = halo_rows(requests)
    me = lax.axis_index("chan")
    pw_slots = [
        lax.dynamic_slice_in_dim(pointwise, ((me - s) % count) * width, width, axis=2)
        for s in range(count)
    ]
    grad_sum = sum(
        jnp.einsum(
            "bco,ohw->bchw", pw_slots[s], cot_full[s * width : (s + 1) * width],
            preferred_element_type=jnp.float32,
        )
        for s in range(count)
    )
    grad_branches = grad_sum.astype(jnp.bfloat16)
    requests = {}
    for which, spacing in enumerate(dilations):
        for side in (-1, 1):
            requests[(which, side * spacing)] = (grad_branches[which + 1], side * spacing)
    grad_halo = halo_rows(requests)

    feat_rows = {0: features.astype(jnp.float32)}
    for offset, rows in feat_halo.items():
        feat_rows[offset] = rows.astype(jnp.float32)
    branches = [features]
    for which, spacing in enumerate(dilations):
        total = jnp.zeros(features.shape, jnp.float32)
        for tap_index in range(9):
            row_step = tap_index // 3 - 1
            col_step = tap_index % 3 - 1
            total = total + kernel[which, tap_index][:, None, None] * jnp.roll(
                feat_rows[row_step * spacing], -col_step * spacing, axis=-1
            )
        branches.append(total.astype(jnp.bfloat16))
    stacked = jnp.stack(branches)

    partial = jnp.einsum(
        "bchw,bco->ohw", stacked, pointwise, preferred_element_type=jnp.float32
    ).astype(jnp.bfloat16)
    result = lax.dynamic_slice_in_dim(partial, me * width, width, axis=0).astype(jnp.float32)
    for s in range(1, count):
        piece = lax.dynamic_slice_in_dim(partial, ((me + s) % count) * width, width, axis=0)
        result = result + chan_shift(piece, s).astype(jnp.float32)
    output = result.astype(jnp.bfloat16)

    point_local = jnp.zeros(pointwise.shape, jnp.float32)
    for s in range(count):
        point_slot = jnp.einsum(
            "bchw,ohw->bco", stacked, cot_full[s * width : (s + 1) * width],
            preferred_element_type=jnp.float32,
        )
        point_local = lax.dynamic_update_slice_in_dim(
            point_local, point_slot, ((me - s) % count) * width, axis=2
        )

    depth_rows = []
    for which, spacing in enumerate(dilations):
        grad_f = grad_branches[which + 1].astype(jnp.float32)
        tap_rows = []
        for tap_index in range(9):
            row_step = tap_index // 3 - 1
            col_step = tap_index % 3 - 1
            tap_rows.append(
                jnp.sum(
                    grad_f * jnp.roll(feat_rows[row_step * spacing], -col_step * spacing, axis=-1),
                    axis=(1, 2),
                )
            )
        depth_rows.append(jnp.stack(tap_rows))
    depth_local = jnp.stack(depth_rows)
    flat = jnp.concatenate([depth_local.reshape(-1), point_local.reshape(-1)])
    flat = band_allreduce(flat)
    depth_total = flat[: depth_local.size].reshape(depth_local.shape)
    point_total = flat[depth_local.size :].reshape(point_local.shape)

    grad_input = grad_branches[0].astype(jnp.float32)
    for which, spacing in enumerate(dilations):
        grad_f = grad_branches[which + 1].astype(jnp.float32)
        for col_step in (-1, 0, 1):
            grad_input = grad_input + kernel[which, 4 + col_step][:, None, None] * jnp.roll(
                grad_f, col_step * spacing, axis=-1
            )
    for which in (0, 2, 1):
        spacing = dilations[which]
        grad_input = lax.optimization_barrier(grad_input)
        for row_step in (-1, 1):
            rows = grad_halo[(which, -row_step * spacing)].astype(jnp.float32)
            for col_step in (-1, 0, 1):
                tap_index = (row_step + 1) * 3 + col_step + 1
                grad_input = grad_input + kernel[which, tap_index][:, None, None] * jnp.roll(
                    rows, col_step * spacing, axis=-1
                )
    return (output, grad_input, depth_total / GSCALE, point_total / GSCALE)


def solution(mesh):
    return jax.shard_map(
        block,
        mesh=mesh,
        in_specs=(
            P("chan", "band", None),
            P(None, None, "chan"),
            P(None, "chan", None),
            P("chan", "band", None),
        ),
        out_specs=(
            P("chan", "band", None),
            P("chan", "band", None),
            P(None, None, "chan"),
            P(None, "chan", None),
        ),
        check_vma=False,
    )
```
